32 devices in a mesh: gx: 8 (over z, core), gy: 4 (over y, x).
Axes of the slice: x: 2, y: 2, z: 4, core: 2. Of those that a mesh axis runs over, the one named last changes fastest.
Arguments:
- pressure: float32 [256, 128, 512], P('gx', 'gy'), may hold values from -6 to 6
- vel_x: float32 [256, 128, 512], P('gx', 'gy'), may hold values from -3 to 3
- vel_y: float32 [256, 128, 512], P('gx', 'gy'), may hold values from -3 to 3
- vel_z: float32 [256, 128, 512], P('gx', 'gy'), may hold values from -3 to 3
- void_frac: float32 [256, 128, 512], P('gx', 'gy'), may hold values from 1e-05 to 0.001
- waves: bfloat16 [24576, 2, 512], P(('gx', 'gy')), may hold values from -6 to 6
- bubble_dest: int32 [24576, 1], P(('gx', 'gy')), may hold values from 0 to 31; in each aligned block of 768 rows (0 to 767, 768 to 1535, ...) at most 48 rows name the same one
- bubble_column: int32 [24576], P(('gx', 'gy')), may hold values from 0 to 1023
- history: bfloat16 [128, 128, 512], P('gx', 'gy'), may hold values from -3 to 3
- delays: int32 [8, 8], replicated, may hold values from 0 to 15
Outputs:
- pressure_out: float32 [256, 128, 512], P('gx', 'gy')
- vel_x_out: float32 [256, 128, 512], P('gx', 'gy')
- vel_y_out: float32 [256, 128, 512], P('gx', 'gy')
- vel_z_out: float32 [256, 128, 512], P('gx', 'gy')
The draws below stay inside these ranges and needn't reach their ends.
Inputs may be any that keep to these rules, and one draw needn't show every extreme that they name: `bubble_dest`: among the 768 bubbles listed on one device (an aligned block of rows), no tile is named more than 48 times.
All inputs are finite; a program needn't handle non-finite values.
Results may differ from the reference program's by a relative error of at most 0.00045.
Values may be sent and summed in bfloat16 or wider, within the bound.
No kernel may reach another device: no remote copies, remote signals or barrier semaphores. Data moves between devices by JAX's collectives and lax.ppermute only.
A program may use at most 128 MiB of HBM per device.

```python
import math
import jax
import jax.numpy as jnp
import numpy as np
from jax import lax

CX = 32
CY = 32
NZ = 512
STEPS = 2
HIST = 16
BUB_DEV = 768
CAP = 48
NX = 256
NY = 128
BUBBLES = 24576
N_GX = 8
N_GY = 4


def set_ends(array, stream_key, smallest, top_value):
    spot = [jax.random.randint(jax.random.fold_in(stream_key, axis), (), 0, length) for axis, length in enumerate(array.shape)]
    main_axis = array.shape.index(max(array.shape))
    next_to = spot[:main_axis] + [(spot[main_axis] + 1) % array.shape[main_axis]] + spot[main_axis + 1:]
    return array.at[tuple(spot)].set(smallest).at[tuple(next_to)].set(top_value)


def block_levels(key, extent, split, low, high):
    factor_of, own = 1.0, jax.random.fold_in(key, 6)
    for position, blocks in split:
        steps = jnp.exp(jax.random.uniform(jax.random.fold_in(own, position), (blocks,), jnp.float32, low / len(split), high / len(split)))
        factor_of = factor_of * jnp.repeat(steps, extent[position] // blocks).reshape([-1 if axis == position else 1 for axis in range(len(extent))])
    return factor_of


def assign_block(stream_key, own, number, rows, amount, top, most, slope):
    ranking = jax.random.permutation(stream_key, amount)
    heavy_load, usual = shares(amount, rows * top, most, slope, True), shares(amount, rows * top, most, slope, False)
    places = jnp.arange(amount)

    def named(lengths, turn):
        used = int((lengths > 0).sum())
        fixed = max(1, used // 4)
        shifted = fixed + (places - fixed + turn * (used - fixed)) % max(1, amount - fixed)
        return jnp.zeros((amount,), jnp.int32).at[ranking[jnp.where(places < fixed, places, shifted)]].set(jnp.asarray(lengths, jnp.int32))

    lengths = jnp.where(number % 4 == 0, named(heavy_load, number // 4), named(usual, number - number // 4 - 1))
    mixed = jax.random.permutation(jax.random.fold_in(own, 3), amount)
    giver, sink = mixed[0:amount // 2 * 2:2], mixed[1:amount // 2 * 2:2]
    room = jnp.minimum(lengths[giver] - 1, most - lengths[sink]) // 2
    room = jnp.where((giver == ranking[0]) | (sink == ranking[0]) | (lengths[sink] == 0), 0, jnp.maximum(room, 0))
    shifted = jax.random.randint(jax.random.fold_in(own, 4), (amount // 2,), 0, 1 << 20) % (room + 1)
    lengths = lengths.at[giver].add(-shifted).at[sink].add(shifted)
    members = jnp.searchsorted(jnp.cumsum(lengths), jnp.arange(rows * top), side="right").astype(jnp.int32)
    listing = members.reshape(top, rows).T
    listing = listing[jax.random.permutation(jax.random.fold_in(own, 1), rows)]
    turn = jax.random.randint(jax.random.fold_in(own, 2), (rows, 1), 0, top)
    return jnp.take_along_axis(listing, (jnp.arange(top)[None, :] + turn) % top, axis=1)


def shares(amount, total, bound, slope, full):
    weights = [(1 << 20) // math.isqrt(standing ** slope) + 1 for standing in range(1, amount + 1)]
    largest = bound if full else min(bound, max(-(-total // amount), total * weights[0] // sum(weights)))
    least = 1 if total - largest >= amount - 1 else 0
    holding, surplus = [largest] + [least] * (amount - 1), total - largest - least * (amount - 1)
    while surplus > 0:
        candidates = [i for i in range(1, amount) if holding[i] < largest] or [i for i in range(1, amount) if holding[i] < bound]
        mass, budget = sum([weights[i] for i in candidates]), surplus
        for i in candidates:
            more = min(bound - holding[i], max(1, budget * weights[i] // mass), surplus)
            holding[i] = holding[i] + more
            surplus = surplus - more
    return np.array(holding)


def scatter_about(key, extent, scale, most, cuts=(), kind=jnp.bfloat16):
    loudness = block_levels(key, extent, cuts, -0.22, 0.18) if cuts else 1.0
    entries = jax.random.normal(key, extent, jnp.float32) * scale * loudness
    return jnp.minimum(jnp.maximum(entries, -most), most).astype(kind)


def setup_inputs(seed: int = 0) -> dict:
    seeds = jax.random.split(jax.random.key(seed), 11)
    pressure = scatter_about(seeds[0], (NX, NY, NZ), 1.0, 6.0, ((0, 8), (1, 4)), jnp.float32)
    vel_x = scatter_about(seeds[1], (NX, NY, NZ), 0.5, 3.0, ((0, 8), (1, 4)), jnp.float32)
    vel_y = scatter_about(seeds[2], (NX, NY, NZ), 0.5, 3.0, ((0, 8), (1, 4)), jnp.float32)
    vel_z = scatter_about(seeds[3], (NX, NY, NZ), 0.5, 3.0, ((0, 8), (1, 4)), jnp.float32)
    void_frac = jnp.clip(jnp.exp(math.log(0.001) - 4.6051703 * jax.random.uniform(seeds[4], (NX, NY, NZ), jnp.float32) ** block_levels(seeds[4], (NX, NY, NZ), ((0, 8), (1, 4)), -0.2, 0.2)), 9.999999747378752e-06, 0.001)
    waves = scatter_about(seeds[5], (BUBBLES, STEPS, NZ), 1.0, 6.0, ((0, 32),))
    bubble_dest_keys = jax.random.split(jax.random.fold_in(seeds[6], 1), BUBBLES // BUB_DEV)
    bubble_dest_turns = jax.random.permutation(jax.random.fold_in(seeds[6], 3), BUBBLES // BUB_DEV)
    bubble_dest = jax.vmap(lambda own, number: assign_block(jax.random.fold_in(seeds[6], 2), own, number, BUB_DEV, N_GX * N_GY, 1, CAP, 2))(bubble_dest_keys, bubble_dest_turns).reshape((BUBBLES, 1))
    bubble_column = set_ends(jax.random.randint(seeds[7], (BUBBLES,), 0, CX * CY), jax.random.fold_in(seeds[7], 1), 0, (CX * CY) - 1).astype(jnp.int32)
    history = scatter_about(seeds[8], (HIST * N_GX, NY, NZ), 0.5, 3.0, ((0, 8), (1, 4)))
    delays = set_ends(jax.random.randint(seeds[9], (N_GX, N_GX), 0, HIST), jax.random.fold_in(seeds[9], 1), 0, HIST - 1).astype(jnp.int32)
    return {"pressure": pressure, "vel_x": vel_x, "vel_y": vel_y, "vel_z": vel_z, "void_frac": void_frac, "waves": waves, "bubble_dest": bubble_dest, "bubble_column": bubble_column, "history": history, "delays": delays}


step_ratio = 0.4
gas_density = 0.001
gas_stiffness = 0.0000529


def material(void_frac):
    liquid = 1.0 - void_frac
    buoyancy = 1.0 / (liquid + void_frac * gas_density)
    stiffness = 1.0 / (liquid + void_frac / gas_stiffness)
    return buoyancy, stiffness


def upper(field, axis):
    rest = lax.slice_in_dim(field, 1, field.shape[axis], axis=axis)
    edge = jnp.zeros_like(lax.slice_in_dim(field, 0, 1, axis=axis))
    return jnp.concatenate([rest, edge], axis)


def lower(field, axis):
    rest = lax.slice_in_dim(field, 0, field.shape[axis] - 1, axis=axis)
    edge = jnp.zeros_like(lax.slice_in_dim(field, 0, 1, axis=axis))
    return jnp.concatenate([edge, rest], axis)


def reference(pressure, vel_x, vel_y, vel_z, void_frac, waves, bubble_dest, bubble_column, history, delays):
    buoyancy, stiffness = material(void_frac)
    dest = bubble_dest[:, 0]
    cell_x = (dest // N_GY) * CX + bubble_column // CY
    cell_y = (dest % N_GY) * CY + bubble_column % CY
    flat = (cell_x * NY + cell_y).astype(jnp.int32)
    source = jnp.zeros((NX * NY, STEPS * NZ), jnp.float32)
    source = source.at[flat].add(waves.reshape(BUBBLES, STEPS * NZ).astype(jnp.float32))
    source = source.reshape(NX, NY, STEPS, NZ)
    panels = history.reshape(N_GX, HIST, NY, NZ)
    cycle = jnp.arange(N_GX, dtype=jnp.int32)

    def one_tile(index):
        dist = jnp.abs(cycle - index)
        dist = jnp.minimum(dist, N_GX - dist)
        weight = 1.0 / (1.0 + 2.0 * dist.astype(jnp.float32) / N_GX)
        rows = panels[cycle, delays[index]].astype(jnp.float32)
        return jnp.tensordot(weight, rows, 1, precision=lax.Precision.HIGHEST)

    incident = lax.map(one_tile, cycle)
    forcing = jnp.zeros((NX, NY, NZ), jnp.float32).at[cycle * CX].set(incident)
    for step in range(STEPS):
        vel_x = vel_x - step_ratio * buoyancy * (upper(pressure, 0) - pressure)
        vel_y = vel_y - step_ratio * buoyancy * (upper(pressure, 1) - pressure)
        vel_z = vel_z - step_ratio * buoyancy * (upper(pressure, 2) - pressure)
        divergence = (vel_x - lower(vel_x, 0)) + (vel_y - lower(vel_y, 1)) + (vel_z - lower(vel_z, 2))
        pressure = pressure + step_ratio * stiffness * (source[:, :, step, :] + forcing - divergence)
    return (pressure, vel_x, vel_y, vel_z)
```

```python
import jax
import jax.numpy as jnp
from jax import lax
from jax.sharding import PartitionSpec as P

step_ratio = 0.4
gas_density = 0.001
gas_stiffness = 5.29e-05


def from_behind(block, axis, distance):
    devices = range(lax.axis_size(axis))
    route = [(i - distance, i) for i in devices if i - distance in devices]
    return lax.ppermute(block, axis, route)


def material(void_frac):
    liquid = 1.0 - void_frac
    buoyancy = 1.0 / (liquid + void_frac * gas_density)
    stiffness = 1.0 / (liquid + void_frac / gas_stiffness)
    return (buoyancy, stiffness)


def bubble_source(waves, bubble_dest, bubble_column, cells):
    tiles_x = lax.axis_size("gx")
    tiles_y = lax.axis_size("gy")
    devices = tiles_x * tiles_y
    bubbles = waves.shape[0]
    steps = waves.shape[1]
    depth = waves.shape[2]
    capacity = 2 * bubbles // devices
    slots = devices * capacity
    me = lax.axis_index("gx") * tiles_y + lax.axis_index("gy")
    dest = bubble_dest[:, 0]
    owners = (dest[:, None] == jnp.arange(devices, dtype=jnp.int32)[None, :]).astype(jnp.int32)
    rank = jnp.sum(jnp.cumsum(owners, axis=0) * owners, axis=1) - 1
    slot_ids = dest * capacity + rank
    placed = slot_ids[None, :] == jnp.arange(slots, dtype=jnp.int32)[:, None]
    outgoing = jnp.dot(
        placed.astype(jnp.bfloat16),
        waves.reshape(bubbles, steps * depth),
        preferred_element_type=jnp.float32,
    ).astype(jnp.bfloat16)
    code = dest * cells + bubble_column
    all_code = lax.all_gather(code, ("gx", "gy"), axis=0, tiled=True).reshape(devices, bubbles)
    all_dest = all_code // cells
    all_col = all_code % cells
    mine = (all_dest == me).astype(jnp.int32)
    in_rank = jnp.cumsum(mine, axis=1) - 1
    in_rank = jnp.where(mine > 0, in_rank, -1)
    slot_of = jnp.arange(capacity, dtype=jnp.int32)
    match = in_rank[:, None, :] == slot_of[None, :, None]
    in_cols = jnp.max(jnp.where(match, all_col[:, None, :] + 1, 0), axis=2) - 1
    incoming = lax.all_to_all(
        outgoing.reshape(devices, capacity, steps * depth),
        ("gx", "gy"),
        split_axis=0,
        concat_axis=0,
        tiled=True,
    )
    hits = (
        jnp.arange(cells, dtype=jnp.int32)[:, None] == in_cols.reshape(slots)[None, :]
    ).astype(jnp.bfloat16)
    source = jnp.dot(
        hits, incoming.reshape(slots, steps * depth), preferred_element_type=jnp.float32
    )
    return source


def incident_plane(history, delays, size_y, depth):
    tiles_x = lax.axis_size("gx")
    my_tile = lax.axis_index("gx")
    cycle = jnp.arange(tiles_x, dtype=jnp.int32)
    dist = jnp.abs(cycle - my_tile)
    dist = jnp.minimum(dist, tiles_x - dist)
    weight = 1.0 / (1.0 + 2.0 * dist.astype(jnp.float32) / tiles_x)
    wanted = lax.dynamic_index_in_dim(delays, my_tile, 1, keepdims=False)
    chosen = jnp.take(history, wanted, axis=0)
    rows = lax.all_to_all(chosen, "gx", split_axis=0, concat_axis=0, tiled=True)
    return jnp.sum(weight[:, None, None] * rows.astype(jnp.float32), axis=0)


def body(
    pressure, vel_x, vel_y, vel_z, void_frac, waves, bubble_dest, bubble_column, history, delays
):
    size_x, size_y, depth = pressure.shape
    steps = waves.shape[1]
    ix = lax.axis_index("gx")
    iy = lax.axis_index("gy")
    has_below_x = ix > 0
    has_below_y = iy > 0
    buoyancy, stiffness = material(void_frac)

    above_x = from_behind(pressure[0:1], "gx", -1)
    above_y = from_behind(pressure[:, 0:1], "gy", -1)
    below_x = from_behind(
        jnp.concatenate([pressure[-1:], vel_x[-1:], void_frac[-1:]], 0), "gx", 1
    )
    below_y = from_behind(
        jnp.concatenate([pressure[:, -1:], vel_y[:, -1:], void_frac[:, -1:]], 1), "gy", 1
    )
    p_bx, vx_bx, void_bx = below_x[0:1], below_x[1:2], below_x[2:3]
    p_by, vy_by, void_by = below_y[:, 0:1], below_y[:, 1:2], below_y[:, 2:3]
    b_bx, _ = material(void_bx)
    b_by, _ = material(void_by)

    source = bubble_source(waves, bubble_dest, bubble_column, size_x * size_y)
    source = source.reshape(size_x, size_y, steps, depth)
    incident = incident_plane(history, delays, size_y, depth)
    forcing = jnp.zeros_like(pressure).at[0].set(incident)
    z_edge = jnp.zeros((size_x, size_y, 1), jnp.float32)

    for step in range(steps):
        next_x = jnp.concatenate([pressure[1:], above_x], 0)
        next_y = jnp.concatenate([pressure[:, 1:], above_y], 1)
        next_z = jnp.concatenate([pressure[:, :, 1:], z_edge], 2)
        vel_x = vel_x - step_ratio * buoyancy * (next_x - pressure)
        vel_y = vel_y - step_ratio * buoyancy * (next_y - pressure)
        vel_z = vel_z - step_ratio * buoyancy * (next_z - pressure)
        vx_bx = vx_bx - step_ratio * b_bx * (pressure[0:1] - p_bx)
        vy_by = vy_by - step_ratio * b_by * (pressure[:, 0:1] - p_by)
        lower_x = jnp.where(has_below_x, vx_bx, 0.0)
        lower_y = jnp.where(has_below_y, vy_by, 0.0)
        prev_x = jnp.concatenate([lower_x, vel_x[:-1]], 0)
        prev_y = jnp.concatenate([lower_y, vel_y[:, :-1]], 1)
        prev_z = jnp.concatenate([z_edge, vel_z[:, :, :-1]], 2)
        divergence = vel_x - prev_x + (vel_y - prev_y) + (vel_z - prev_z)
        pressure = pressure + step_ratio * stiffness * (
            source[:, :, step, :] + forcing - divergence
        )
        if step + 1 < steps:
            above_x = from_behind(pressure[0:1], "gx", -1)
            above_y = from_behind(pressure[:, 0:1], "gy", -1)
            p_bx = from_behind(pressure[-1:], "gx", 1)
            p_by = from_behind(pressure[:, -1:], "gy", 1)
    return (pressure, vel_x, vel_y, vel_z)


def solution(mesh):
    in_specs = (
        P("gx", "gy", None),
        P("gx", "gy", None),
        P("gx", "gy", None),
        P("gx", "gy", None),
        P("gx", "gy", None),
        P(("gx", "gy"), None, None),
        P(("gx", "gy"), None),
        P(("gx", "gy")),
        P("gx", "gy", None),
        P(),
    )
    out_specs = (P("gx", "gy", None), P("gx", "gy", None), P("gx", "gy", None), P("gx", "gy", None))
    return jax.shard_map(body, mesh=mesh, in_specs=in_specs, out_specs=out_specs, check_vma=False)
```

```python
import jax
import jax.numpy as jnp
from jax import lax
from jax.sharding import PartitionSpec as P

step_ratio = 0.4
gas_density = 0.001
gas_stiffness = 5.29e-05


def from_behind(block, axis, distance):
    devices = range(lax.axis_size(axis))
    route = [(i - distance, i) for i in devices if i - distance in devices]
    return lax.ppermute(block, axis, route)


def material(void_frac):
    liquid = 1.0 - void_frac
    buoyancy = 1.0 / (liquid + void_frac * gas_density)
    stiffness = 1.0 / (liquid + void_frac / gas_stiffness)
    return (buoyancy, stiffness)


def bubble_source(waves, bubble_dest, bubble_column, cells, ready):
    tiles_x = lax.axis_size("gx")
    tiles_y = lax.axis_size("gy")
    devices = tiles_x * tiles_y
    bubbles = waves.shape[0]
    steps = waves.shape[1]
    depth = waves.shape[2]
    capacity = 2 * bubbles // devices
    slots = devices * capacity
    me = lax.axis_index("gx") * tiles_y + lax.axis_index("gy")
    dest = bubble_dest[:, 0]
    owners = (dest[:, None] == jnp.arange(devices, dtype=jnp.int32)[None, :]).astype(jnp.int32)
    rank = jnp.sum(jnp.cumsum(owners, axis=0) * owners, axis=1) - 1
    slot_ids = dest * capacity + rank
    placed = slot_ids[None, :] == jnp.arange(slots, dtype=jnp.int32)[:, None]
    outgoing = jnp.dot(
        placed.astype(jnp.bfloat16),
        waves.reshape(bubbles, steps * depth),
        preferred_element_type=jnp.float32,
    ).astype(jnp.bfloat16)
    code = dest * cells + bubble_column
    all_code = lax.all_gather(code, ("gx", "gy"), axis=0, tiled=True).reshape(devices, bubbles)
    all_dest = all_code // cells
    all_col = all_code % cells
    mine = (all_dest == me).astype(jnp.int32)
    in_rank = jnp.cumsum(mine, axis=1) - 1
    in_rank = jnp.where(mine > 0, in_rank, -1)
    slot_of = jnp.arange(capacity, dtype=jnp.int32)
    match = in_rank[:, None, :] == slot_of[None, :, None]
    in_cols = jnp.max(jnp.where(match, all_col[:, None, :] + 1, 0), axis=2) - 1
    in_cols, outgoing, ready = lax.optimization_barrier((in_cols, outgoing, ready))
    incoming = lax.all_to_all(
        outgoing.reshape(devices, capacity, steps * depth),
        ("gx", "gy"),
        split_axis=0,
        concat_axis=0,
        tiled=True,
    )
    hits = (
        jnp.arange(cells, dtype=jnp.int32)[:, None] == in_cols.reshape(slots)[None, :]
    ).astype(jnp.bfloat16)
    source = jnp.dot(
        hits, incoming.reshape(slots, steps * depth), preferred_element_type=jnp.float32
    )
    return source, ready


def incident_plane(history, delays, size_y, depth):
    tiles_x = lax.axis_size("gx")
    my_tile = lax.axis_index("gx")
    cycle = jnp.arange(tiles_x, dtype=jnp.int32)
    dist = jnp.abs(cycle - my_tile)
    dist = jnp.minimum(dist, tiles_x - dist)
    weight = 1.0 / (1.0 + 2.0 * dist.astype(jnp.float32) / tiles_x)
    wanted = lax.dynamic_index_in_dim(delays, my_tile, 1, keepdims=False)
    chosen = jnp.take(history, wanted, axis=0)
    rows = lax.all_to_all(chosen, "gx", split_axis=0, concat_axis=0, tiled=True)
    return jnp.sum(weight[:, None, None] * rows.astype(jnp.float32), axis=0)


def body(
    pressure, vel_x, vel_y, vel_z, void_frac, waves, bubble_dest, bubble_column, history, delays
):
    size_x, size_y, depth = pressure.shape
    steps = waves.shape[1]
    ix = lax.axis_index("gx")
    iy = lax.axis_index("gy")
    has_below_x = ix > 0
    has_below_y = iy > 0
    buoyancy, stiffness = material(void_frac)

    above_x = from_behind(pressure[0:1], "gx", -1)
    above_y = from_behind(pressure[:, 0:1], "gy", -1)
    below_x = from_behind(
        jnp.concatenate([pressure[-1:], vel_x[-1:], void_frac[-1:]], 0), "gx", 1
    )
    below_y = from_behind(
        jnp.concatenate([pressure[:, -1:], vel_y[:, -1:], void_frac[:, -1:]], 1), "gy", 1
    )

    incident = incident_plane(history, delays, size_y, depth)
    ready = (above_x, above_y, below_x, below_y, incident)
    source, ready = bubble_source(waves, bubble_dest, bubble_column, size_x * size_y, ready)
    above_x, above_y, below_x, below_y, incident = ready
    source = source.reshape(size_x, size_y, steps, depth)
    p_bx, vx_bx, void_bx = below_x[0:1], below_x[1:2], below_x[2:3]
    p_by, vy_by, void_by = below_y[:, 0:1], below_y[:, 1:2], below_y[:, 2:3]
    b_bx, _ = material(void_bx)
    b_by, _ = material(void_by)
    forcing = jnp.zeros_like(pressure).at[0].set(incident)
    z_edge = jnp.zeros((size_x, size_y, 1), jnp.float32)

    for step in range(steps):
        next_x = jnp.concatenate([pressure[1:], above_x], 0)
        next_y = jnp.concatenate([pressure[:, 1:], above_y], 1)
        next_z = jnp.concatenate([pressure[:, :, 1:], z_edge], 2)
        vel_x = vel_x - step_ratio * buoyancy * (next_x - pressure)
        vel_y = vel_y - step_ratio * buoyancy * (next_y - pressure)
        vel_z = vel_z - step_ratio * buoyancy * (next_z - pressure)
        vx_bx = vx_bx - step_ratio * b_bx * (pressure[0:1] - p_bx)
        vy_by = vy_by - step_ratio * b_by * (pressure[:, 0:1] - p_by)
        lower_x = jnp.where(has_below_x, vx_bx, 0.0)
        lower_y = jnp.where(has_below_y, vy_by, 0.0)
        prev_x = jnp.concatenate([lower_x, vel_x[:-1]], 0)
        prev_y = jnp.concatenate([lower_y, vel_y[:, :-1]], 1)
        prev_z = jnp.concatenate([z_edge, vel_z[:, :, :-1]], 2)
        divergence = vel_x - prev_x + (vel_y - prev_y) + (vel_z - prev_z)
        pressure = pressure + step_ratio * stiffness * (
            source[:, :, step, :] + forcing - divergence
        )
        if step + 1 < steps:
            above_x = from_behind(pressure[0:1], "gx", -1)
            above_y = from_behind(pressure[:, 0:1], "gy", -1)
            p_bx = from_behind(pressure[-1:], "gx", 1)
            p_by = from_behind(pressure[:, -1:], "gy", 1)
    return (pressure, vel_x, vel_y, vel_z)


def solution(mesh):
    in_specs = (
        P("gx", "gy", None),
        P("gx", "gy", None),
        P("gx", "gy", None),
        P("gx", "gy", None),
        P("gx", "gy", None),
        P(("gx", "gy"), None, None),
        P(("gx", "gy"), None),
        P(("gx", "gy")),
        P("gx", "gy", None),
        P(),
    )
    out_specs = (P("gx", "gy", None), P("gx", "gy", None), P("gx", "gy", None), P("gx", "gy", None))
    return jax.shard_map(body, mesh=mesh, in_specs=in_specs, out_specs=out_specs, check_vma=False)
```

```python
import jax
import jax.numpy as jnp
from jax import lax
from jax.sharding import PartitionSpec as P

step_ratio = 0.4
gas_density = 0.001
gas_stiffness = 5.29e-05


def from_behind(block, axis, distance):
    devices = range(lax.axis_size(axis))
    route = [(i - distance, i) for i in devices if i - distance in devices]
    return lax.ppermute(block, axis, route)


def material(void_frac):
    liquid = 1.0 - void_frac
    buoyancy = 1.0 / (liquid + void_frac * gas_density)
    stiffness = 1.0 / (liquid + void_frac / gas_stiffness)
    return (buoyancy, stiffness)


def bubble_source(waves, bubble_dest, bubble_column, cells, ready):
    tiles_x = lax.axis_size("gx")
    tiles_y = lax.axis_size("gy")
    devices = tiles_x * tiles_y
    bubbles = waves.shape[0]
    steps = waves.shape[1]
    depth = waves.shape[2]
    capacity = 2 * bubbles // devices
    slots = devices * capacity
    dest = bubble_dest[:, 0]
    owners = (dest[:, None] == jnp.arange(devices, dtype=jnp.int32)[None, :]).astype(jnp.int32)
    rank = jnp.sum(jnp.cumsum(owners, axis=0) * owners, axis=1) - 1
    slot_ids = dest * capacity + rank
    placed = slot_ids[None, :] == jnp.arange(slots, dtype=jnp.int32)[:, None]
    outgoing = jnp.dot(
        placed.astype(jnp.bfloat16),
        waves.reshape(bubbles, steps * depth),
        preferred_element_type=jnp.float32,
    ).astype(jnp.bfloat16)
    out_cols = jnp.max(jnp.where(placed, bubble_column[None, :] + 1, 0), axis=1) - 1
    in_cols = lax.all_to_all(
        out_cols.reshape(devices, capacity),
        ("gx", "gy"),
        split_axis=0,
        concat_axis=0,
        tiled=True,
    )
    in_cols, outgoing, ready = lax.optimization_barrier((in_cols, outgoing, ready))
    incoming = lax.all_to_all(
        outgoing.reshape(devices, capacity, steps * depth),
        ("gx", "gy"),
        split_axis=0,
        concat_axis=0,
        tiled=True,
    )
    hits = (
        jnp.arange(cells, dtype=jnp.int32)[:, None] == in_cols.reshape(slots)[None, :]
    ).astype(jnp.bfloat16)
    source = jnp.dot(
        hits, incoming.reshape(slots, steps * depth), preferred_element_type=jnp.float32
    )
    return source, ready


def incident_plane(history, delays, size_y, depth):
    tiles_x = lax.axis_size("gx")
    my_tile = lax.axis_index("gx")
    cycle = jnp.arange(tiles_x, dtype=jnp.int32)
    dist = jnp.abs(cycle - my_tile)
    dist = jnp.minimum(dist, tiles_x - dist)
    weight = 1.0 / (1.0 + 2.0 * dist.astype(jnp.float32) / tiles_x)
    wanted = lax.dynamic_index_in_dim(delays, my_tile, 1, keepdims=False)
    chosen = jnp.take(history, wanted, axis=0)
    rows = lax.all_to_all(chosen, "gx", split_axis=0, concat_axis=0, tiled=True)
    return jnp.sum(weight[:, None, None] * rows.astype(jnp.float32), axis=0)


def body(
    pressure, vel_x, vel_y, vel_z, void_frac, waves, bubble_dest, bubble_column, history, delays
):
    size_x, size_y, depth = pressure.shape
    steps = waves.shape[1]
    ix = lax.axis_index("gx")
    iy = lax.axis_index("gy")
    has_below_x = ix > 0
    has_below_y = iy > 0
    buoyancy, stiffness = material(void_frac)

    above_x = from_behind(pressure[0:1], "gx", -1)
    above_y = from_behind(pressure[:, 0:1], "gy", -1)
    below_x = from_behind(
        jnp.concatenate([pressure[-1:], vel_x[-1:], void_frac[-1:]], 0), "gx", 1
    )
    below_y = from_behind(
        jnp.concatenate([pressure[:, -1:], vel_y[:, -1:], void_frac[:, -1:]], 1), "gy", 1
    )

    ready = (above_x, above_y, below_x, below_y)
    source, ready = bubble_source(waves, bubble_dest, bubble_column, size_x * size_y, ready)
    above_x, above_y, below_x, below_y = ready
    incident = incident_plane(history, delays, size_y, depth)
    source = source.reshape(size_x, size_y, steps, depth)
    p_bx, vx_bx, void_bx = below_x[0:1], below_x[1:2], below_x[2:3]
    p_by, vy_by, void_by = below_y[:, 0:1], below_y[:, 1:2], below_y[:, 2:3]
    b_bx, _ = material(void_bx)
    b_by, _ = material(void_by)
    forcing = jnp.zeros_like(pressure).at[0].set(incident)
    z_edge = jnp.zeros((size_x, size_y, 1), jnp.float32)

    for step in range(steps):
        next_x = jnp.concatenate([pressure[1:], above_x], 0)
        next_y = jnp.concatenate([pressure[:, 1:], above_y], 1)
        next_z = jnp.concatenate([pressure[:, :, 1:], z_edge], 2)
        vel_x = vel_x - step_ratio * buoyancy * (next_x - pressure)
        vel_y = vel_y - step_ratio * buoyancy * (next_y - pressure)
        vel_z = vel_z - step_ratio * buoyancy * (next_z - pressure)
        vx_bx = vx_bx - step_ratio * b_bx * (pressure[0:1] - p_bx)
        vy_by = vy_by - step_ratio * b_by * (pressure[:, 0:1] - p_by)
        lower_x = jnp.where(has_below_x, vx_bx, 0.0)
        lower_y = jnp.where(has_below_y, vy_by, 0.0)
        prev_x = jnp.concatenate([lower_x, vel_x[:-1]], 0)
        prev_y = jnp.concatenate([lower_y, vel_y[:, :-1]], 1)
        prev_z = jnp.concatenate([z_edge, vel_z[:, :, :-1]], 2)
        divergence = vel_x - prev_x + (vel_y - prev_y) + (vel_z - prev_z)
        pressure = pressure + step_ratio * stiffness * (
            source[:, :, step, :] + forcing - divergence
        )
        if step + 1 < steps:
            above_x = from_behind(pressure[0:1], "gx", -1)
            above_y = from_behind(pressure[:, 0:1], "gy", -1)
            p_bx = from_behind(pressure[-1:], "gx", 1)
            p_by = from_behind(pressure[:, -1:], "gy", 1)
    return (pressure, vel_x, vel_y, vel_z)


def solution(mesh):
    in_specs = (
        P("gx", "gy", None),
        P("gx", "gy", None),
        P("gx", "gy", None),
        P("gx", "gy", None),
        P("gx", "gy", None),
        P(("gx", "gy"), None, None),
        P(("gx", "gy"), None),
        P(("gx", "gy")),
        P("gx", "gy", None),
        P(),
    )
    out_specs = (P("gx", "gy", None), P("gx", "gy", None), P("gx", "gy", None), P("gx", "gy", None))
    return jax.shard_map(body, mesh=mesh, in_specs=in_specs, out_specs=out_specs, check_vma=False)
```

```python
import jax
import jax.numpy as jnp
from jax import lax
from jax.sharding import PartitionSpec as P

step_ratio = 0.4
gas_density = 0.001
gas_stiffness = 5.29e-05


def from_behind(block, axis, distance):
    devices = range(lax.axis_size(axis))
    route = [(i - distance, i) for i in devices if i - distance in devices]
    return lax.ppermute(block, axis, route)


def material(void_frac):
    liquid = 1.0 - void_frac
    buoyancy = 1.0 / (liquid + void_frac * gas_density)
    stiffness = 1.0 / (liquid + void_frac / gas_stiffness)
    return (buoyancy, stiffness)


def bubble_source(waves, bubble_dest, bubble_column, cells):
    tiles_x = lax.axis_size("gx")
    tiles_y = lax.axis_size("gy")
    devices = tiles_x * tiles_y
    bubbles = waves.shape[0]
    steps = waves.shape[1]
    depth = waves.shape[2]
    capacity = 2 * bubbles // devices
    slots = devices * capacity
    dest = bubble_dest[:, 0]
    owners = (dest[:, None] == jnp.arange(devices, dtype=jnp.int32)[None, :]).astype(jnp.int32)
    rank = jnp.sum(jnp.cumsum(owners, axis=0) * owners, axis=1) - 1
    slot_ids = dest * capacity + rank
    placed = slot_ids[None, :] == jnp.arange(slots, dtype=jnp.int32)[:, None]
    outgoing = jnp.dot(
        placed.astype(jnp.bfloat16),
        waves.reshape(bubbles, steps * depth),
        preferred_element_type=jnp.float32,
    ).astype(jnp.bfloat16)
    out_cols = jnp.max(jnp.where(placed, bubble_column[None, :] + 1, 0), axis=1) - 1
    in_cols = lax.all_to_all(
        out_cols.reshape(devices, capacity),
        ("gx", "gy"),
        split_axis=0,
        concat_axis=0,
        tiled=True,
    )
    hits = (
        jnp.arange(cells, dtype=jnp.int32)[:, None] == in_cols.reshape(slots)[None, :]
    ).astype(jnp.bfloat16)
    outgoing = outgoing.reshape(devices, capacity, steps, depth)
    return hits, outgoing


def exchange(sending):
    return lax.all_to_all(sending, ("gx", "gy"), split_axis=0, concat_axis=0, tiled=True)


def incident_plane(history, delays, size_y, depth):
    tiles_x = lax.axis_size("gx")
    my_tile = lax.axis_index("gx")
    cycle = jnp.arange(tiles_x, dtype=jnp.int32)
    dist = jnp.abs(cycle - my_tile)
    dist = jnp.minimum(dist, tiles_x - dist)
    weight = 1.0 / (1.0 + 2.0 * dist.astype(jnp.float32) / tiles_x)
    wanted = lax.dynamic_index_in_dim(delays, my_tile, 1, keepdims=False)
    chosen = jnp.take(history, wanted, axis=0)
    rows = lax.all_to_all(chosen, "gx", split_axis=0, concat_axis=0, tiled=True)
    return jnp.sum(weight[:, None, None] * rows.astype(jnp.float32), axis=0)


def body(
    pressure, vel_x, vel_y, vel_z, void_frac, waves, bubble_dest, bubble_column, history, delays
):
    size_x, size_y, depth = pressure.shape
    steps = waves.shape[1]
    ix = lax.axis_index("gx")
    iy = lax.axis_index("gy")
    has_below_x = ix > 0
    has_below_y = iy > 0
    buoyancy, stiffness = material(void_frac)

    above_x = from_behind(pressure[0:1], "gx", -1)
    above_y = from_behind(pressure[:, 0:1], "gy", -1)
    below_x = from_behind(
        jnp.concatenate([pressure[-1:], vel_x[-1:], void_frac[-1:]], 0), "gx", 1
    )
    below_y = from_behind(
        jnp.concatenate([pressure[:, -1:], vel_y[:, -1:], void_frac[:, -1:]], 1), "gy", 1
    )

    hits, outgoing = bubble_source(waves, bubble_dest, bubble_column, size_x * size_y)
    slots = hits.shape[1]
    incident = incident_plane(history, delays, size_y, depth)
    p_bx, vx_bx, void_bx = below_x[0:1], below_x[1:2], below_x[2:3]
    p_by, vy_by, void_by = below_y[:, 0:1], below_y[:, 1:2], below_y[:, 2:3]
    b_bx, _ = material(void_bx)
    b_by, _ = material(void_by)
    forcing = jnp.zeros_like(pressure).at[0].set(incident)
    z_edge = jnp.zeros((size_x, size_y, 1), jnp.float32)

    sending = outgoing[:, :, 0, :]
    for step in range(steps):
        incoming = exchange(sending)
        next_x = jnp.concatenate([pressure[1:], above_x], 0)
        next_y = jnp.concatenate([pressure[:, 1:], above_y], 1)
        next_z = jnp.concatenate([pressure[:, :, 1:], z_edge], 2)
        vel_x = vel_x - step_ratio * buoyancy * (next_x - pressure)
        vel_y = vel_y - step_ratio * buoyancy * (next_y - pressure)
        vel_z = vel_z - step_ratio * buoyancy * (next_z - pressure)
        vx_bx = vx_bx - step_ratio * b_bx * (pressure[0:1] - p_bx)
        vy_by = vy_by - step_ratio * b_by * (pressure[:, 0:1] - p_by)
        lower_x = jnp.where(has_below_x, vx_bx, 0.0)
        lower_y = jnp.where(has_below_y, vy_by, 0.0)
        prev_x = jnp.concatenate([lower_x, vel_x[:-1]], 0)
        prev_y = jnp.concatenate([lower_y, vel_y[:, :-1]], 1)
        prev_z = jnp.concatenate([z_edge, vel_z[:, :, :-1]], 2)
        divergence = vel_x - prev_x + (vel_y - prev_y) + (vel_z - prev_z)
        rest = forcing - divergence
        incoming, vel_x, vel_y, vel_z, vx_bx, vy_by, rest = lax.optimization_barrier(
            (incoming, vel_x, vel_y, vel_z, vx_bx, vy_by, rest)
        )
        source = jnp.dot(hits, incoming.reshape(slots, depth), preferred_element_type=jnp.float32)
        source = source.reshape(size_x, size_y, depth)
        pressure = pressure + step_ratio * stiffness * (source + rest)
        if step + 1 < steps:
            sending, pressure = lax.optimization_barrier((outgoing[:, :, step + 1, :], pressure))
            above_x = from_behind(pressure[0:1], "gx", -1)
            above_y = from_behind(pressure[:, 0:1], "gy", -1)
            p_bx = from_behind(pressure[-1:], "gx", 1)
            p_by = from_behind(pressure[:, -1:], "gy", 1)
    return (pressure, vel_x, vel_y, vel_z)


def solution(mesh):
    in_specs = (
        P("gx", "gy", None),
        P("gx", "gy", None),
        P("gx", "gy", None),
        P("gx", "gy", None),
        P("gx", "gy", None),
        P(("gx", "gy"), None, None),
        P(("gx", "gy"), None),
        P(("gx", "gy")),
        P("gx", "gy", None),
        P(),
    )
    out_specs = (P("gx", "gy", None), P("gx", "gy", None), P("gx", "gy", None), P("gx", "gy", None))
    return jax.shard_map(body, mesh=mesh, in_specs=in_specs, out_specs=out_specs, check_vma=False)
```

```python
import jax
import jax.numpy as jnp
from jax import lax
from jax.sharding import PartitionSpec as P

step_ratio = 0.4
gas_density = 0.001
gas_stiffness = 5.29e-05


def from_behind(block, axis, distance):
    devices = range(lax.axis_size(axis))
    route = [(i - distance, i) for i in devices if i - distance in devices]
    return lax.ppermute(block, axis, route)


def material(void_frac):
    liquid = 1.0 - void_frac
    buoyancy = 1.0 / (liquid + void_frac * gas_density)
    stiffness = 1.0 / (liquid + void_frac / gas_stiffness)
    return (buoyancy, stiffness)


def bubble_source(waves, bubble_dest, bubble_column, cells, ready):
    tiles_x = lax.axis_size("gx")
    tiles_y = lax.axis_size("gy")
    devices = tiles_x * tiles_y
    bubbles = waves.shape[0]
    steps = waves.shape[1]
    depth = waves.shape[2]
    capacity = 2 * bubbles // devices
    slots = devices * capacity
    dest = bubble_dest[:, 0]
    owners = (dest[:, None] == jnp.arange(devices, dtype=jnp.int32)[None, :]).astype(jnp.int32)
    rank = jnp.sum(jnp.cumsum(owners, axis=0) * owners, axis=1) - 1
    slot_ids = dest * capacity + rank
    placed = slot_ids[None, :] == jnp.arange(slots, dtype=jnp.int32)[:, None]
    outgoing = jnp.dot(
        placed.astype(jnp.bfloat16),
        waves.reshape(bubbles, steps * depth),
        preferred_element_type=jnp.float32,
    ).astype(jnp.bfloat16)
    out_cols = jnp.max(jnp.where(placed, bubble_column[None, :] + 1, 0), axis=1) - 1
    in_cols = lax.all_to_all(
        out_cols.reshape(devices, capacity),
        ("gx", "gy"),
        split_axis=0,
        concat_axis=0,
        tiled=True,
    )
    incoming = lax.all_to_all(
        outgoing.reshape(devices, capacity, steps * depth),
        ("gx", "gy"),
        split_axis=0,
        concat_axis=0,
        tiled=True,
    )
    hits = (
        jnp.arange(cells, dtype=jnp.int32)[:, None] == in_cols.reshape(slots)[None, :]
    ).astype(jnp.bfloat16)
    source = jnp.dot(
        hits, incoming.reshape(slots, steps * depth), preferred_element_type=jnp.float32
    )
    return source, ready


def incident_plane(history, delays):
    tiles_x = lax.axis_size("gx")
    my_tile = lax.axis_index("gx")
    shifts = jnp.arange(tiles_x, dtype=jnp.int32)
    dist = jnp.minimum(shifts, tiles_x - shifts)
    weight = 1.0 / (1.0 + 2.0 * dist.astype(jnp.float32) / tiles_x)
    readers = (my_tile + shifts) % tiles_x
    wanted = jnp.take(lax.dynamic_index_in_dim(delays, my_tile, 1, keepdims=False), readers)
    chosen = jnp.take(history, wanted, axis=0)
    total = weight[0] * chosen[0].astype(jnp.float32)
    for shift in range(1, tiles_x):
        route = [(j, (j + shift) % tiles_x) for j in range(tiles_x)]
        got = lax.ppermute(chosen[shift], "gx", route)
        total = total + weight[shift] * got.astype(jnp.float32)
    return total


def body(
    pressure, vel_x, vel_y, vel_z, void_frac, waves, bubble_dest, bubble_column, history, delays
):
    size_x, size_y, depth = pressure.shape
    steps = waves.shape[1]
    ix = lax.axis_index("gx")
    iy = lax.axis_index("gy")
    has_below_x = ix > 0
    has_below_y = iy > 0
    buoyancy, stiffness = material(void_frac)

    above_x = from_behind(pressure[0:1], "gx", -1)
    above_y = from_behind(pressure[:, 0:1], "gy", -1)
    below_x = from_behind(
        jnp.concatenate([pressure[-1:], vel_x[-1:], void_frac[-1:]], 0), "gx", 1
    )
    below_y = from_behind(
        jnp.concatenate([pressure[:, -1:], vel_y[:, -1:], void_frac[:, -1:]], 1), "gy", 1
    )

    ready = (above_x, above_y, below_x, below_y)
    source, ready = bubble_source(waves, bubble_dest, bubble_column, size_x * size_y, ready)
    above_x, above_y, below_x, below_y = ready
    incident = incident_plane(history, delays)
    source = source.reshape(size_x, size_y, steps, depth)
    p_bx, vx_bx, void_bx = below_x[0:1], below_x[1:2], below_x[2:3]
    p_by, vy_by, void_by = below_y[:, 0:1], below_y[:, 1:2], below_y[:, 2:3]
    b_bx, _ = material(void_bx)
    b_by, _ = material(void_by)
    forcing = jnp.zeros_like(pressure).at[0].set(incident)
    z_edge = jnp.zeros((size_x, size_y, 1), jnp.float32)

    for step in range(steps):
        next_x = jnp.concatenate([pressure[1:], above_x], 0)
        next_y = jnp.concatenate([pressure[:, 1:], above_y], 1)
        next_z = jnp.concatenate([pressure[:, :, 1:], z_edge], 2)
        vel_x = vel_x - step_ratio * buoyancy * (next_x - pressure)
        vel_y = vel_y - step_ratio * buoyancy * (next_y - pressure)
        vel_z = vel_z - step_ratio * buoyancy * (next_z - pressure)
        vx_bx = vx_bx - step_ratio * b_bx * (pressure[0:1] - p_bx)
        vy_by = vy_by - step_ratio * b_by * (pressure[:, 0:1] - p_by)
        lower_x = jnp.where(has_below_x, vx_bx, 0.0)
        lower_y = jnp.where(has_below_y, vy_by, 0.0)
        prev_x = jnp.concatenate([lower_x, vel_x[:-1]], 0)
        prev_y = jnp.concatenate([lower_y, vel_y[:, :-1]], 1)
        prev_z = jnp.concatenate([z_edge, vel_z[:, :, :-1]], 2)
        divergence = vel_x - prev_x + (vel_y - prev_y) + (vel_z - prev_z)
        pressure = pressure + step_ratio * stiffness * (
            source[:, :, step, :] + forcing - divergence
        )
        if step + 1 < steps:
            above_x = from_behind(pressure[0:1], "gx", -1)
            above_y = from_behind(pressure[:, 0:1], "gy", -1)
            p_bx = from_behind(pressure[-1:], "gx", 1)
            p_by = from_behind(pressure[:, -1:], "gy", 1)
    return (pressure, vel_x, vel_y, vel_z)


def solution(mesh):
    in_specs = (
        P("gx", "gy", None),
        P("gx", "gy", None),
        P("gx", "gy", None),
        P("gx", "gy", None),
        P("gx", "gy", None),
        P(("gx", "gy"), None, None),
        P(("gx", "gy"), None),
        P(("gx", "gy")),
        P("gx", "gy", None),
        P(),
    )
    out_specs = (P("gx", "gy", None), P("gx", "gy", None), P("gx", "gy", None), P("gx", "gy", None))
    return jax.shard_map(body, mesh=mesh, in_specs=in_specs, out_specs=out_specs, check_vma=False)
```

```python
import jax
import jax.numpy as jnp
from jax import lax
from jax.sharding import PartitionSpec as P

step_ratio = 0.4
gas_density = 0.001
gas_stiffness = 5.29e-05


def from_behind(block, axis, distance):
    devices = range(lax.axis_size(axis))
    route = [(i - distance, i) for i in devices if i - distance in devices]
    return lax.ppermute(block, axis, route)


def material(void_frac):
    liquid = 1.0 - void_frac
    buoyancy = 1.0 / (liquid + void_frac * gas_density)
    stiffness = 1.0 / (liquid + void_frac / gas_stiffness)
    return (buoyancy, stiffness)


def bubble_source(waves, bubble_dest, bubble_column, cells, ready):
    tiles_x = lax.axis_size("gx")
    tiles_y = lax.axis_size("gy")
    devices = tiles_x * tiles_y
    bubbles = waves.shape[0]
    steps = waves.shape[1]
    depth = waves.shape[2]
    capacity = 2 * bubbles // devices
    slots = devices * capacity
    dest = bubble_dest[:, 0]
    owners = (dest[:, None] == jnp.arange(devices, dtype=jnp.int32)[None, :]).astype(jnp.int32)
    rank = jnp.sum(jnp.cumsum(owners, axis=0) * owners, axis=1) - 1
    slot_ids = dest * capacity + rank
    placed = slot_ids[None, :] == jnp.arange(slots, dtype=jnp.int32)[:, None]
    listed = jnp.arange(bubbles, dtype=jnp.int32)
    holder = jnp.max(jnp.where(placed, listed[None, :] + 1, 0), axis=1) - 1
    outgoing = jnp.take(waves.reshape(bubbles, steps * depth), jnp.maximum(holder, 0), axis=0)
    out_cols = jnp.where(holder >= 0, jnp.take(bubble_column, jnp.maximum(holder, 0)), -1)
    in_cols = lax.all_to_all(
        out_cols.reshape(devices, capacity),
        ("gx", "gy"),
        split_axis=0,
        concat_axis=0,
        tiled=True,
    )
    in_cols, outgoing, ready = lax.optimization_barrier((in_cols, outgoing, ready))
    incoming = lax.all_to_all(
        outgoing.reshape(devices, capacity, steps * depth),
        ("gx", "gy"),
        split_axis=0,
        concat_axis=0,
        tiled=True,
    )
    hits = (
        jnp.arange(cells, dtype=jnp.int32)[:, None] == in_cols.reshape(slots)[None, :]
    ).astype(jnp.bfloat16)
    source = jnp.dot(
        hits, incoming.reshape(slots, steps * depth), preferred_element_type=jnp.float32
    )
    return source, ready


def incident_plane(history, delays, size_y, depth):
    tiles_x = lax.axis_size("gx")
    my_tile = lax.axis_index("gx")
    cycle = jnp.arange(tiles_x, dtype=jnp.int32)
    dist = jnp.abs(cycle - my_tile)
    dist = jnp.minimum(dist, tiles_x - dist)
    weight = 1.0 / (1.0 + 2.0 * dist.astype(jnp.float32) / tiles_x)
    wanted = lax.dynamic_index_in_dim(delays, my_tile, 1, keepdims=False)
    chosen = jnp.take(history, wanted, axis=0)
    rows = lax.all_to_all(chosen, "gx", split_axis=0, concat_axis=0, tiled=True)
    return jnp.sum(weight[:, None, None] * rows.astype(jnp.float32), axis=0)


def body(
    pressure, vel_x, vel_y, vel_z, void_frac, waves, bubble_dest, bubble_column, history, delays
):
    size_x, size_y, depth = pressure.shape
    steps = waves.shape[1]
    ix = lax.axis_index("gx")
    iy = lax.axis_index("gy")
    has_below_x = ix > 0
    has_below_y = iy > 0
    buoyancy, stiffness = material(void_frac)

    above_x = from_behind(pressure[0:1], "gx", -1)
    above_y = from_behind(pressure[:, 0:1], "gy", -1)
    below_x = from_behind(
        jnp.concatenate([pressure[-1:], vel_x[-1:], void_frac[-1:]], 0), "gx", 1
    )
    below_y = from_behind(
        jnp.concatenate([pressure[:, -1:], vel_y[:, -1:], void_frac[:, -1:]], 1), "gy", 1
    )

    ready = (above_x, above_y, below_x, below_y)
    source, ready = bubble_source(waves, bubble_dest, bubble_column, size_x * size_y, ready)
    above_x, above_y, below_x, below_y = ready
    incident = incident_plane(history, delays, size_y, depth)
    source = source.reshape(size_x, size_y, steps, depth)
    p_bx, vx_bx, void_bx = below_x[0:1], below_x[1:2], below_x[2:3]
    p_by, vy_by, void_by = below_y[:, 0:1], below_y[:, 1:2], below_y[:, 2:3]
    b_bx, _ = material(void_bx)
    b_by, _ = material(void_by)
    forcing = jnp.zeros_like(pressure).at[0].set(incident)
    z_edge = jnp.zeros((size_x, size_y, 1), jnp.float32)

    for step in range(steps):
        next_x = jnp.concatenate([pressure[1:], above_x], 0)
        next_y = jnp.concatenate([pressure[:, 1:], above_y], 1)
        next_z = jnp.concatenate([pressure[:, :, 1:], z_edge], 2)
        vel_x = vel_x - step_ratio * buoyancy * (next_x - pressure)
        vel_y = vel_y - step_ratio * buoyancy * (next_y - pressure)
        vel_z = vel_z - step_ratio * buoyancy * (next_z - pressure)
        vx_bx = vx_bx - step_ratio * b_bx * (pressure[0:1] - p_bx)
        vy_by = vy_by - step_ratio * b_by * (pressure[:, 0:1] - p_by)
        lower_x = jnp.where(has_below_x, vx_bx, 0.0)
        lower_y = jnp.where(has_below_y, vy_by, 0.0)
        prev_x = jnp.concatenate([lower_x, vel_x[:-1]], 0)
        prev_y = jnp.concatenate([lower_y, vel_y[:, :-1]], 1)
        prev_z = jnp.concatenate([z_edge, vel_z[:, :, :-1]], 2)
        divergence = vel_x - prev_x + (vel_y - prev_y) + (vel_z - prev_z)
        pressure = pressure + step_ratio * stiffness * (
            source[:, :, step, :] + forcing - divergence
        )
        if step + 1 < steps:
            above_x = from_behind(pressure[0:1], "gx", -1)
            above_y = from_behind(pressure[:, 0:1], "gy", -1)
            p_bx = from_behind(pressure[-1:], "gx", 1)
            p_by = from_behind(pressure[:, -1:], "gy", 1)
    return (pressure, vel_x, vel_y, vel_z)


def solution(mesh):
    in_specs = (
        P("gx", "gy", None),
        P("gx", "gy", None),
        P("gx", "gy", None),
        P("gx", "gy", None),
        P("gx", "gy", None),
        P(("gx", "gy"), None, None),
        P(("gx", "gy"), None),
        P(("gx", "gy")),
        P("gx", "gy", None),
        P(),
    )
    out_specs = (P("gx", "gy", None), P("gx", "gy", None), P("gx", "gy", None), P("gx", "gy", None))
    return jax.shard_map(body, mesh=mesh, in_specs=in_specs, out_specs=out_specs, check_vma=False)
```

```python
import jax
import jax.numpy as jnp
from jax import lax
from jax.sharding import PartitionSpec as P

step_ratio = 0.4
gas_density = 0.001
gas_stiffness = 5.29e-05


def from_behind(block, axis, distance):
    devices = range(lax.axis_size(axis))
    route = [(i - distance, i) for i in devices if i - distance in devices]
    return lax.ppermute(block, axis, route)


def material(void_frac):
    liquid = 1.0 - void_frac
    buoyancy = 1.0 / (liquid + void_frac * gas_density)
    stiffness = 1.0 / (liquid + void_frac / gas_stiffness)
    return (buoyancy, stiffness)


def bubble_source(waves, bubble_dest, bubble_column, cells, ready):
    tiles_x = lax.axis_size("gx")
    tiles_y = lax.axis_size("gy")
    devices = tiles_x * tiles_y
    bubbles = waves.shape[0]
    steps = waves.shape[1]
    depth = waves.shape[2]
    capacity = 2 * bubbles // devices
    slots = devices * capacity
    dest = bubble_dest[:, 0]
    owners = (dest[:, None] == jnp.arange(devices, dtype=jnp.int32)[None, :]).astype(jnp.int32)
    rank = jnp.sum(jnp.cumsum(owners, axis=0) * owners, axis=1) - 1
    slot_ids = dest * capacity + rank
    placed = slot_ids[None, :] == jnp.arange(slots, dtype=jnp.int32)[:, None]
    outgoing = jnp.dot(
        placed.astype(jnp.bfloat16),
        waves.reshape(bubbles, steps * depth),
        preferred_element_type=jnp.float32,
    ).astype(jnp.bfloat16)
    out_cols = jnp.max(jnp.where(placed, bubble_column[None, :] + 1, 0), axis=1) - 1
    in_cols = lax.all_to_all(
        out_cols.reshape(devices, capacity),
        ("gx", "gy"),
        split_axis=0,
        concat_axis=0,
        tiled=True,
    )
    in_cols, outgoing, ready = lax.optimization_barrier((in_cols, outgoing, ready))
    incoming = lax.all_to_all(
        outgoing.reshape(devices, capacity, steps * depth),
        ("gx", "gy"),
        split_axis=0,
        concat_axis=0,
        tiled=True,
    )
    hits = (
        jnp.arange(cells, dtype=jnp.int32)[:, None] == in_cols.reshape(slots)[None, :]
    ).astype(jnp.bfloat16)
    return hits, incoming.reshape(slots, steps, depth), ready


def incident_plane(history, delays, size_y, depth):
    tiles_x = lax.axis_size("gx")
    my_tile = lax.axis_index("gx")
    cycle = jnp.arange(tiles_x, dtype=jnp.int32)
    dist = jnp.abs(cycle - my_tile)
    dist = jnp.minimum(dist, tiles_x - dist)
    weight = 1.0 / (1.0 + 2.0 * dist.astype(jnp.float32) / tiles_x)
    wanted = lax.dynamic_index_in_dim(delays, my_tile, 1, keepdims=False)
    chosen = jnp.take(history, wanted, axis=0)
    rows = lax.all_to_all(chosen, "gx", split_axis=0, concat_axis=0, tiled=True)
    return jnp.sum(weight[:, None, None] * rows.astype(jnp.float32), axis=0)


def body(
    pressure, vel_x, vel_y, vel_z, void_frac, waves, bubble_dest, bubble_column, history, delays
):
    size_x, size_y, depth = pressure.shape
    steps = waves.shape[1]
    ix = lax.axis_index("gx")
    iy = lax.axis_index("gy")
    has_below_x = ix > 0
    has_below_y = iy > 0
    buoyancy, stiffness = material(void_frac)

    above_x = from_behind(pressure[0:1], "gx", -1)
    above_y = from_behind(pressure[:, 0:1], "gy", -1)
    below_x = from_behind(
        jnp.concatenate([pressure[-1:], vel_x[-1:], void_frac[-1:]], 0), "gx", 1
    )
    below_y = from_behind(
        jnp.concatenate([pressure[:, -1:], vel_y[:, -1:], void_frac[:, -1:]], 1), "gy", 1
    )

    ready = (above_x, above_y, below_x, below_y)
    hits, incoming, ready = bubble_source(
        waves, bubble_dest, bubble_column, size_x * size_y, ready
    )
    above_x, above_y, below_x, below_y = ready
    history, _ = lax.optimization_barrier((history, incoming))
    incident = incident_plane(history, delays, size_y, depth)
    p_bx, vx_bx, void_bx = below_x[0:1], below_x[1:2], below_x[2:3]
    p_by, vy_by, void_by = below_y[:, 0:1], below_y[:, 1:2], below_y[:, 2:3]
    b_bx, _ = material(void_bx)
    b_by, _ = material(void_by)
    forcing = jnp.zeros_like(pressure).at[0].set(incident)
    z_edge = jnp.zeros((size_x, size_y, 1), jnp.float32)

    wave_rows = incoming
    for step in range(steps):
        source = jnp.dot(hits, wave_rows[:, step, :], preferred_element_type=jnp.float32)
        source = source.reshape(size_x, size_y, depth)
        next_x = jnp.concatenate([pressure[1:], above_x], 0)
        next_y = jnp.concatenate([pressure[:, 1:], above_y], 1)
        next_z = jnp.concatenate([pressure[:, :, 1:], z_edge], 2)
        vel_x = vel_x - step_ratio * buoyancy * (next_x - pressure)
        vel_y = vel_y - step_ratio * buoyancy * (next_y - pressure)
        vel_z = vel_z - step_ratio * buoyancy * (next_z - pressure)
        vx_bx = vx_bx - step_ratio * b_bx * (pressure[0:1] - p_bx)
        vy_by = vy_by - step_ratio * b_by * (pressure[:, 0:1] - p_by)
        lower_x = jnp.where(has_below_x, vx_bx, 0.0)
        lower_y = jnp.where(has_below_y, vy_by, 0.0)
        prev_x = jnp.concatenate([lower_x, vel_x[:-1]], 0)
        prev_y = jnp.concatenate([lower_y, vel_y[:, :-1]], 1)
        prev_z = jnp.concatenate([z_edge, vel_z[:, :, :-1]], 2)
        divergence = vel_x - prev_x + (vel_y - prev_y) + (vel_z - prev_z)
        pressure = pressure + step_ratio * stiffness * (
            source + forcing - divergence
        )
        if step + 1 < steps:
            wave_rows, pressure = lax.optimization_barrier((wave_rows, pressure))
            above_x = from_behind(pressure[0:1], "gx", -1)
            above_y = from_behind(pressure[:, 0:1], "gy", -1)
            p_bx = from_behind(pressure[-1:], "gx", 1)
            p_by = from_behind(pressure[:, -1:], "gy", 1)
    return (pressure, vel_x, vel_y, vel_z)


def solution(mesh):
    in_specs = (
        P("gx", "gy", None),
        P("gx", "gy", None),
        P("gx", "gy", None),
        P("gx", "gy", None),
        P("gx", "gy", None),
        P(("gx", "gy"), None, None),
        P(("gx", "gy"), None),
        P(("gx", "gy")),
        P("gx", "gy", None),
        P(),
    )
    out_specs = (P("gx", "gy", None), P("gx", "gy", None), P("gx", "gy", None), P("gx", "gy", None))
    return jax.shard_map(body, mesh=mesh, in_specs=in_specs, out_specs=out_specs, check_vma=False)
```

```python
import jax
import jax.numpy as jnp
from jax import lax
from jax.sharding import PartitionSpec as P

step_ratio = 0.4
gas_density = 0.001
gas_stiffness = 5.29e-05


def from_behind(block, axis, distance):
    devices = range(lax.axis_size(axis))
    route = [(i - distance, i) for i in devices if i - distance in devices]
    return lax.ppermute(block, axis, route)


def material(void_frac):
    liquid = 1.0 - void_frac
    buoyancy = 1.0 / (liquid + void_frac * gas_density)
    stiffness = 1.0 / (liquid + void_frac / gas_stiffness)
    return (buoyancy, stiffness)


def bubble_source(waves, bubble_dest, bubble_column, cells, ready):
    tiles_x = lax.axis_size("gx")
    tiles_y = lax.axis_size("gy")
    devices = tiles_x * tiles_y
    bubbles = waves.shape[0]
    steps = waves.shape[1]
    depth = waves.shape[2]
    capacity = 2 * bubbles // devices
    slots = devices * capacity
    dest = bubble_dest[:, 0]
    owners = (dest[:, None] == jnp.arange(devices, dtype=jnp.int32)[None, :]).astype(jnp.int32)
    rank = jnp.sum(jnp.cumsum(owners, axis=0) * owners, axis=1) - 1
    slot_ids = dest * capacity + rank
    placed = slot_ids[None, :] == jnp.arange(slots, dtype=jnp.int32)[:, None]
    outgoing = jnp.dot(
        placed.astype(jnp.bfloat16),
        waves.reshape(bubbles, steps * depth),
        preferred_element_type=jnp.float32,
    ).astype(jnp.bfloat16)
    out_cols = jnp.max(jnp.where(placed, bubble_column[None, :] + 1, 0), axis=1) - 1
    in_cols = lax.all_to_all(
        out_cols.reshape(devices, capacity),
        ("gx", "gy"),
        split_axis=0,
        concat_axis=0,
        tiled=True,
    )
    in_cols, outgoing, ready = lax.optimization_barrier((in_cols, outgoing, ready))
    incoming = lax.all_to_all(
        outgoing.reshape(devices, capacity, steps * depth),
        ("gx", "gy"),
        split_axis=0,
        concat_axis=0,
        tiled=True,
    )
    hits = (
        jnp.arange(cells, dtype=jnp.int32)[:, None] == in_cols.reshape(slots)[None, :]
    ).astype(jnp.bfloat16)
    source = jnp.dot(
        hits, incoming.reshape(slots, steps * depth), preferred_element_type=jnp.float32
    )
    return source, incoming, ready


def incident_plane(history, delays, size_y, depth):
    tiles_x = lax.axis_size("gx")
    my_tile = lax.axis_index("gx")
    cycle = jnp.arange(tiles_x, dtype=jnp.int32)
    dist = jnp.abs(cycle - my_tile)
    dist = jnp.minimum(dist, tiles_x - dist)
    weight = 1.0 / (1.0 + 2.0 * dist.astype(jnp.float32) / tiles_x)
    wanted = lax.dynamic_index_in_dim(delays, my_tile, 1, keepdims=False)
    chosen = jnp.take(history, wanted, axis=0)
    rows = lax.all_to_all(chosen, "gx", split_axis=0, concat_axis=0, tiled=True)
    return jnp.sum(weight[:, None, None] * rows.astype(jnp.float32), axis=0)


def body(
    pressure, vel_x, vel_y, vel_z, void_frac, waves, bubble_dest, bubble_column, history, delays
):
    size_x, size_y, depth = pressure.shape
    steps = waves.shape[1]
    ix = lax.axis_index("gx")
    iy = lax.axis_index("gy")
    has_below_x = ix > 0
    has_below_y = iy > 0
    buoyancy, stiffness = material(void_frac)

    above_x = from_behind(pressure[0:1], "gx", -1)
    above_y = from_behind(pressure[:, 0:1], "gy", -1)
    below_x = from_behind(
        jnp.concatenate([pressure[-1:], vel_x[-1:], void_frac[-1:]], 0), "gx", 1
    )
    below_y = from_behind(
        jnp.concatenate([pressure[:, -1:], vel_y[:, -1:], void_frac[:, -1:]], 1), "gy", 1
    )

    ready = (above_x, above_y, below_x, below_y)
    source, incoming, ready = bubble_source(
        waves, bubble_dest, bubble_column, size_x * size_y, ready
    )
    above_x, above_y, below_x, below_y = ready
    history, _ = lax.optimization_barrier((history, incoming))
    incident = incident_plane(history, delays, size_y, depth)
    source = source.reshape(size_x, size_y, steps, depth)
    p_bx, vx_bx, void_bx = below_x[0:1], below_x[1:2], below_x[2:3]
    p_by, vy_by, void_by = below_y[:, 0:1], below_y[:, 1:2], below_y[:, 2:3]
    b_bx, _ = material(void_bx)
    b_by, _ = material(void_by)
    forcing = jnp.zeros_like(pressure).at[0].set(incident)
    z_edge = jnp.zeros((size_x, size_y, 1), jnp.float32)

    for step in range(steps):
        next_x = jnp.concatenate([pressure[1:], above_x], 0)
        next_y = jnp.concatenate([pressure[:, 1:], above_y], 1)
        next_z = jnp.concatenate([pressure[:, :, 1:], z_edge], 2)
        vel_x = vel_x - step_ratio * buoyancy * (next_x - pressure)
        vel_y = vel_y - step_ratio * buoyancy * (next_y - pressure)
        vel_z = vel_z - step_ratio * buoyancy * (next_z - pressure)
        vx_bx = vx_bx - step_ratio * b_bx * (pressure[0:1] - p_bx)
        vy_by = vy_by - step_ratio * b_by * (pressure[:, 0:1] - p_by)
        lower_x = jnp.where(has_below_x, vx_bx, 0.0)
        lower_y = jnp.where(has_below_y, vy_by, 0.0)
        prev_x = jnp.concatenate([lower_x, vel_x[:-1]], 0)
        prev_y = jnp.concatenate([lower_y, vel_y[:, :-1]], 1)
        prev_z = jnp.concatenate([z_edge, vel_z[:, :, :-1]], 2)
        divergence = vel_x - prev_x + (vel_y - prev_y) + (vel_z - prev_z)
        pressure = pressure + step_ratio * stiffness * (
            source[:, :, step, :] + forcing - divergence
        )
        if step + 1 < steps:
            above_x = from_behind(pressure[0:1], "gx", -1)
            above_y = from_behind(pressure[:, 0:1], "gy", -1)
            p_bx = from_behind(pressure[-1:], "gx", 1)
            p_by = from_behind(pressure[:, -1:], "gy", 1)
    return (pressure, vel_x, vel_y, vel_z)


def solution(mesh):
    in_specs = (
        P("gx", "gy", None),
        P("gx", "gy", None),
        P("gx", "gy", None),
        P("gx", "gy", None),
        P("gx", "gy", None),
        P(("gx", "gy"), None, None),
        P(("gx", "gy"), None),
        P(("gx", "gy")),
        P("gx", "gy", None),
        P(),
    )
    out_specs = (P("gx", "gy", None), P("gx", "gy", None), P("gx", "gy", None), P("gx", "gy", None))
    return jax.shard_map(body, mesh=mesh, in_specs=in_specs, out_specs=out_specs, check_vma=False)
```

```python
import jax
import jax.numpy as jnp
from jax import lax
from jax.sharding import PartitionSpec as P

step_ratio = 0.4
gas_density = 0.001
gas_stiffness = 5.29e-05


def from_behind(block, axis, distance):
    devices = range(lax.axis_size(axis))
    route = [(i - distance, i) for i in devices if i - distance in devices]
    return lax.ppermute(block, axis, route)


def material(void_frac):
    liquid = 1.0 - void_frac
    buoyancy = 1.0 / (liquid + void_frac * gas_density)
    stiffness = 1.0 / (liquid + void_frac / gas_stiffness)
    return (buoyancy, stiffness)


def bubble_source(waves, bubble_dest, bubble_column, cells, ready):
    tiles_x = lax.axis_size("gx")
    tiles_y = lax.axis_size("gy")
    devices = tiles_x * tiles_y
    bubbles = waves.shape[0]
    steps = waves.shape[1]
    depth = waves.shape[2]
    capacity = 2 * bubbles // devices
    slots = devices * capacity
    dest = bubble_dest[:, 0]
    owners = (dest[:, None] == jnp.arange(devices, dtype=jnp.int32)[None, :]).astype(jnp.int32)
    rank = jnp.sum(jnp.cumsum(owners, axis=0) * owners, axis=1) - 1
    slot_ids = dest * capacity + rank
    placed = slot_ids[None, :] == jnp.arange(slots, dtype=jnp.int32)[:, None]
    outgoing = jnp.dot(
        placed.astype(jnp.bfloat16),
        waves.reshape(bubbles, steps * depth),
        preferred_element_type=jnp.float32,
    ).astype(jnp.bfloat16)
    out_cols = jnp.max(jnp.where(placed, bubble_column[None, :] + 1, 0), axis=1) - 1
    in_cols = lax.all_to_all(
        out_cols.reshape(devices, capacity),
        ("gx", "gy"),
        split_axis=0,
        concat_axis=0,
        tiled=True,
    )
    incoming = lax.all_to_all(
        outgoing.reshape(devices, capacity, steps * depth),
        ("gx", "gy"),
        split_axis=0,
        concat_axis=0,
        tiled=True,
    )
    hits = (
        jnp.arange(cells, dtype=jnp.int32)[:, None] == in_cols.reshape(slots)[None, :]
    ).astype(jnp.bfloat16)
    source = jnp.dot(
        hits, incoming.reshape(slots, steps * depth), preferred_element_type=jnp.float32
    )
    return source, ready


def incident_plane(history, delays, size_y, depth):
    tiles_x = lax.axis_size("gx")
    my_tile = lax.axis_index("gx")
    cycle = jnp.arange(tiles_x, dtype=jnp.int32)
    dist = jnp.abs(cycle - my_tile)
    dist = jnp.minimum(dist, tiles_x - dist)
    weight = 1.0 / (1.0 + 2.0 * dist.astype(jnp.float32) / tiles_x)
    wanted = lax.dynamic_index_in_dim(delays, my_tile, 1, keepdims=False)
    chosen = jnp.take(history, wanted, axis=0)
    rows = lax.all_to_all(chosen, "gx", split_axis=0, concat_axis=0, tiled=True)
    return jnp.sum(weight[:, None, None] * rows.astype(jnp.float32), axis=0)


def body(
    pressure, vel_x, vel_y, vel_z, void_frac, waves, bubble_dest, bubble_column, history, delays
):
    size_x, size_y, depth = pressure.shape
    steps = waves.shape[1]
    ix = lax.axis_index("gx")
    iy = lax.axis_index("gy")
    has_below_x = ix > 0
    has_below_y = iy > 0
    buoyancy, stiffness = material(void_frac)

    above_x = from_behind(pressure[0:1], "gx", -1)
    above_y = from_behind(pressure[:, 0:1], "gy", -1)
    below_x = from_behind(
        jnp.concatenate([pressure[-1:], vel_x[-1:], void_frac[-1:]], 0), "gx", 1
    )
    below_y = from_behind(
        jnp.concatenate([pressure[:, -1:], vel_y[:, -1:], void_frac[:, -1:]], 1), "gy", 1
    )

    ready = (above_x, above_y, below_x, below_y)
    source, ready = bubble_source(waves, bubble_dest, bubble_column, size_x * size_y, ready)
    above_x, above_y, below_x, below_y = ready
    incident = incident_plane(history, delays, size_y, depth)
    source = source.reshape(size_x, size_y, steps, depth)
    p_bx, vx_bx, void_bx = below_x[0:1], below_x[1:2], below_x[2:3]
    p_by, vy_by, void_by = below_y[:, 0:1], below_y[:, 1:2], below_y[:, 2:3]
    b_bx, _ = material(void_bx)
    b_by, _ = material(void_by)
    forcing = jnp.zeros_like(pressure).at[0].set(incident)
    z_edge = jnp.zeros((size_x, size_y, 1), jnp.float32)

    for step in range(steps):
        next_x = jnp.concatenate([pressure[1:], above_x], 0)
        next_y = jnp.concatenate([pressure[:, 1:], above_y], 1)
        next_z = jnp.concatenate([pressure[:, :, 1:], z_edge], 2)
        vel_x = vel_x - step_ratio * buoyancy * (next_x - pressure)
        vel_y = vel_y - step_ratio * buoyancy * (next_y - pressure)
        vel_z = vel_z - step_ratio * buoyancy * (next_z - pressure)
        vx_bx = vx_bx - step_ratio * b_bx * (pressure[0:1] - p_bx)
        vy_by = vy_by - step_ratio * b_by * (pressure[:, 0:1] - p_by)
        lower_x = jnp.where(has_below_x, vx_bx, 0.0)
        lower_y = jnp.where(has_below_y, vy_by, 0.0)
        prev_x = jnp.concatenate([lower_x, vel_x[:-1]], 0)
        prev_y = jnp.concatenate([lower_y, vel_y[:, :-1]], 1)
        prev_z = jnp.concatenate([z_edge, vel_z[:, :, :-1]], 2)
        divergence = vel_x - prev_x + (vel_y - prev_y) + (vel_z - prev_z)
        pressure = pressure + step_ratio * stiffness * (
            source[:, :, step, :] + forcing - divergence
        )
        if step + 1 < steps:
            above_x = from_behind(pressure[0:1], "gx", -1)
            above_y = from_behind(pressure[:, 0:1], "gy", -1)
            p_bx = from_behind(pressure[-1:], "gx", 1)
            p_by = from_behind(pressure[:, -1:], "gy", 1)
    return (pressure, vel_x, vel_y, vel_z)


def solution(mesh):
    in_specs = (
        P("gx", "gy", None),
        P("gx", "gy", None),
        P("gx", "gy", None),
        P("gx", "gy", None),
        P("gx", "gy", None),
        P(("gx", "gy"), None, None),
        P(("gx", "gy"), None),
        P(("gx", "gy")),
        P("gx", "gy", None),
        P(),
    )
    out_specs = (P("gx", "gy", None), P("gx", "gy", None), P("gx", "gy", None), P("gx", "gy", None))
    return jax.shard_map(body, mesh=mesh, in_specs=in_specs, out_specs=out_specs, check_vma=False)
```

```python
import jax
import jax.numpy as jnp
from jax import lax
from jax.sharding import PartitionSpec as P

step_ratio = 0.4
gas_density = 0.001
gas_stiffness = 5.29e-05


def from_behind(block, axis, distance):
    devices = range(lax.axis_size(axis))
    route = [(i - distance, i) for i in devices if i - distance in devices]
    return lax.ppermute(block, axis, route)


def y_plane_from_behind(plane, axis, distance):
    return from_behind(plane, axis, distance)[:, None, :]


def material(void_frac):
    liquid = 1.0 - void_frac
    buoyancy = 1.0 / (liquid + void_frac * gas_density)
    stiffness = 1.0 / (liquid + void_frac / gas_stiffness)
    return (buoyancy, stiffness)


def bubble_source(waves, bubble_dest, bubble_column, cells, ready):
    tiles_x = lax.axis_size("gx")
    tiles_y = lax.axis_size("gy")
    devices = tiles_x * tiles_y
    bubbles = waves.shape[0]
    steps = waves.shape[1]
    depth = waves.shape[2]
    capacity = 2 * bubbles // devices
    slots = devices * capacity
    dest = bubble_dest[:, 0]
    owners = (dest[:, None] == jnp.arange(devices, dtype=jnp.int32)[None, :]).astype(jnp.int32)
    rank = jnp.sum(jnp.cumsum(owners, axis=0) * owners, axis=1) - 1
    slot_ids = dest * capacity + rank
    placed = slot_ids[None, :] == jnp.arange(slots, dtype=jnp.int32)[:, None]
    outgoing = jnp.dot(
        placed.astype(jnp.bfloat16),
        waves.reshape(bubbles, steps * depth),
        preferred_element_type=jnp.float32,
    ).astype(jnp.bfloat16)
    out_cols = jnp.max(jnp.where(placed, bubble_column[None, :] + 1, 0), axis=1) - 1
    in_cols = lax.all_to_all(
        out_cols.reshape(devices, capacity),
        ("gx", "gy"),
        split_axis=0,
        concat_axis=0,
        tiled=True,
    )
    in_cols, outgoing, ready = lax.optimization_barrier((in_cols, outgoing, ready))
    incoming = lax.all_to_all(
        outgoing.reshape(devices, capacity, steps * depth),
        ("gx", "gy"),
        split_axis=0,
        concat_axis=0,
        tiled=True,
    )
    hits = (
        jnp.arange(cells, dtype=jnp.int32)[:, None] == in_cols.reshape(slots)[None, :]
    ).astype(jnp.bfloat16)
    source = jnp.dot(
        hits, incoming.reshape(slots, steps * depth), preferred_element_type=jnp.float32
    )
    return source, ready


def incident_plane(history, delays, size_y, depth):
    tiles_x = lax.axis_size("gx")
    my_tile = lax.axis_index("gx")
    cycle = jnp.arange(tiles_x, dtype=jnp.int32)
    dist = jnp.abs(cycle - my_tile)
    dist = jnp.minimum(dist, tiles_x - dist)
    weight = 1.0 / (1.0 + 2.0 * dist.astype(jnp.float32) / tiles_x)
    wanted = lax.dynamic_index_in_dim(delays, my_tile, 1, keepdims=False)
    chosen = jnp.take(history, wanted, axis=0)
    rows = lax.all_to_all(chosen, "gx", split_axis=0, concat_axis=0, tiled=True)
    return jnp.sum(weight[:, None, None] * rows.astype(jnp.float32), axis=0)


def body(
    pressure, vel_x, vel_y, vel_z, void_frac, waves, bubble_dest, bubble_column, history, delays
):
    size_x, size_y, depth = pressure.shape
    steps = waves.shape[1]
    ix = lax.axis_index("gx")
    iy = lax.axis_index("gy")
    has_below_x = ix > 0
    has_below_y = iy > 0
    buoyancy, stiffness = material(void_frac)

    above_x = from_behind(pressure[0:1], "gx", -1)
    above_y = y_plane_from_behind(pressure[:, 0], "gy", -1)
    below_x = from_behind(
        jnp.concatenate([pressure[-1:], vel_x[-1:], void_frac[-1:]], 0), "gx", 1
    )
    below_y = from_behind(
        jnp.stack([pressure[:, -1], vel_y[:, -1], void_frac[:, -1]], 0), "gy", 1
    )
    below_y = jnp.moveaxis(below_y, 0, 1)

    ready = (above_x, above_y, below_x, below_y)
    source, ready = bubble_source(waves, bubble_dest, bubble_column, size_x * size_y, ready)
    above_x, above_y, below_x, below_y = ready
    incident = incident_plane(history, delays, size_y, depth)
    source = source.reshape(size_x, size_y, steps, depth)
    p_bx, vx_bx, void_bx = below_x[0:1], below_x[1:2], below_x[2:3]
    p_by, vy_by, void_by = below_y[:, 0:1], below_y[:, 1:2], below_y[:, 2:3]
    b_bx, _ = material(void_bx)
    b_by, _ = material(void_by)
    forcing = jnp.zeros_like(pressure).at[0].set(incident)
    z_edge = jnp.zeros((size_x, size_y, 1), jnp.float32)

    for step in range(steps):
        next_x = jnp.concatenate([pressure[1:], above_x], 0)
        next_y = jnp.concatenate([pressure[:, 1:], above_y], 1)
        next_z = jnp.concatenate([pressure[:, :, 1:], z_edge], 2)
        vel_x = vel_x - step_ratio * buoyancy * (next_x - pressure)
        vel_y = vel_y - step_ratio * buoyancy * (next_y - pressure)
        vel_z = vel_z - step_ratio * buoyancy * (next_z - pressure)
        vx_bx = vx_bx - step_ratio * b_bx * (pressure[0:1] - p_bx)
        vy_by = vy_by - step_ratio * b_by * (pressure[:, 0:1] - p_by)
        lower_x = jnp.where(has_below_x, vx_bx, 0.0)
        lower_y = jnp.where(has_below_y, vy_by, 0.0)
        prev_x = jnp.concatenate([lower_x, vel_x[:-1]], 0)
        prev_y = jnp.concatenate([lower_y, vel_y[:, :-1]], 1)
        prev_z = jnp.concatenate([z_edge, vel_z[:, :, :-1]], 2)
        divergence = vel_x - prev_x + (vel_y - prev_y) + (vel_z - prev_z)
        pressure = pressure + step_ratio * stiffness * (
            source[:, :, step, :] + forcing - divergence
        )
        if step + 1 < steps:
            above_x = from_behind(pressure[0:1], "gx", -1)
            above_y = y_plane_from_behind(pressure[:, 0], "gy", -1)
            p_bx = from_behind(pressure[-1:], "gx", 1)
            p_by = y_plane_from_behind(pressure[:, -1], "gy", 1)
    return (pressure, vel_x, vel_y, vel_z)


def solution(mesh):
    in_specs = (
        P("gx", "gy", None),
        P("gx", "gy", None),
        P("gx", "gy", None),
        P("gx", "gy", None),
        P("gx", "gy", None),
        P(("gx", "gy"), None, None),
        P(("gx", "gy"), None),
        P(("gx", "gy")),
        P("gx", "gy", None),
        P(),
    )
    out_specs = (P("gx", "gy", None), P("gx", "gy", None), P("gx", "gy", None), P("gx", "gy", None))
    return jax.shard_map(body, mesh=mesh, in_specs=in_specs, out_specs=out_specs, check_vma=False)
```

```python
import jax
import jax.numpy as jnp
from jax import lax
from jax.sharding import PartitionSpec as P

step_ratio = 0.4
gas_density = 0.001
gas_stiffness = 5.29e-05


def from_behind(block, axis, distance):
    devices = range(lax.axis_size(axis))
    route = [(i - distance, i) for i in devices if i - distance in devices]
    sent = lax.ppermute(block.astype(jnp.bfloat16), axis, route)
    return sent.astype(jnp.float32)


def y_plane_from_behind(plane, axis, distance):
    return from_behind(plane, axis, distance)[:, None, :]


def material(void_frac):
    liquid = 1.0 - void_frac
    buoyancy = 1.0 / (liquid + void_frac * gas_density)
    stiffness = 1.0 / (liquid + void_frac / gas_stiffness)
    return (buoyancy, stiffness)


def bubble_source(waves, bubble_dest, bubble_column, cells, ready):
    tiles_x = lax.axis_size("gx")
    tiles_y = lax.axis_size("gy")
    devices = tiles_x * tiles_y
    bubbles = waves.shape[0]
    steps = waves.shape[1]
    depth = waves.shape[2]
    capacity = 2 * bubbles // devices
    slots = devices * capacity
    dest = bubble_dest[:, 0]
    owners = (dest[:, None] == jnp.arange(devices, dtype=jnp.int32)[None, :]).astype(jnp.int32)
    rank = jnp.sum(jnp.cumsum(owners, axis=0) * owners, axis=1) - 1
    slot_ids = dest * capacity + rank
    placed = slot_ids[None, :] == jnp.arange(slots, dtype=jnp.int32)[:, None]
    outgoing = jnp.dot(
        placed.astype(jnp.bfloat16),
        waves.reshape(bubbles, steps * depth),
        preferred_element_type=jnp.float32,
    ).astype(jnp.bfloat16)
    out_cols = jnp.max(jnp.where(placed, bubble_column[None, :] + 1, 0), axis=1) - 1
    in_cols = lax.all_to_all(
        out_cols.reshape(devices, capacity),
        ("gx", "gy"),
        split_axis=0,
        concat_axis=0,
        tiled=True,
    )
    in_cols, outgoing, ready = lax.optimization_barrier((in_cols, outgoing, ready))
    incoming = lax.all_to_all(
        outgoing.reshape(devices, capacity, steps * depth),
        ("gx", "gy"),
        split_axis=0,
        concat_axis=0,
        tiled=True,
    )
    hits = (
        jnp.arange(cells, dtype=jnp.int32)[:, None] == in_cols.reshape(slots)[None, :]
    ).astype(jnp.bfloat16)
    source = jnp.dot(
        hits, incoming.reshape(slots, steps * depth), preferred_element_type=jnp.float32
    )
    return source, ready


def incident_plane(history, delays, size_y, depth):
    tiles_x = lax.axis_size("gx")
    my_tile = lax.axis_index("gx")
    cycle = jnp.arange(tiles_x, dtype=jnp.int32)
    dist = jnp.abs(cycle - my_tile)
    dist = jnp.minimum(dist, tiles_x - dist)
    weight = 1.0 / (1.0 + 2.0 * dist.astype(jnp.float32) / tiles_x)
    wanted = lax.dynamic_index_in_dim(delays, my_tile, 1, keepdims=False)
    chosen = jnp.take(history, wanted, axis=0)
    rows = lax.all_to_all(chosen, "gx", split_axis=0, concat_axis=0, tiled=True)
    return jnp.sum(weight[:, None, None] * rows.astype(jnp.float32), axis=0)


def body(
    pressure, vel_x, vel_y, vel_z, void_frac, waves, bubble_dest, bubble_column, history, delays
):
    size_x, size_y, depth = pressure.shape
    steps = waves.shape[1]
    ix = lax.axis_index("gx")
    iy = lax.axis_index("gy")
    has_below_x = ix > 0
    has_below_y = iy > 0
    buoyancy, stiffness = material(void_frac)

    above_x = from_behind(pressure[0:1], "gx", -1)
    above_y = y_plane_from_behind(pressure[:, 0], "gy", -1)
    below_x = from_behind(
        jnp.concatenate([pressure[-1:], vel_x[-1:], void_frac[-1:]], 0), "gx", 1
    )
    below_y = from_behind(
        jnp.stack([pressure[:, -1], vel_y[:, -1], void_frac[:, -1]], 0), "gy", 1
    )
    below_y = jnp.moveaxis(below_y, 0, 1)

    ready = (above_x, above_y, below_x, below_y)
    source, ready = bubble_source(waves, bubble_dest, bubble_column, size_x * size_y, ready)
    above_x, above_y, below_x, below_y = ready
    incident = incident_plane(history, delays, size_y, depth)
    source = source.reshape(size_x, size_y, steps, depth)
    p_bx, vx_bx, void_bx = below_x[0:1], below_x[1:2], below_x[2:3]
    p_by, vy_by, void_by = below_y[:, 0:1], below_y[:, 1:2], below_y[:, 2:3]
    b_bx, _ = material(void_bx)
    b_by, _ = material(void_by)
    forcing = jnp.zeros_like(pressure).at[0].set(incident)
    z_edge = jnp.zeros((size_x, size_y, 1), jnp.float32)

    for step in range(steps):
        next_x = jnp.concatenate([pressure[1:], above_x], 0)
        next_y = jnp.concatenate([pressure[:, 1:], above_y], 1)
        next_z = jnp.concatenate([pressure[:, :, 1:], z_edge], 2)
        vel_x = vel_x - step_ratio * buoyancy * (next_x - pressure)
        vel_y = vel_y - step_ratio * buoyancy * (next_y - pressure)
        vel_z = vel_z - step_ratio * buoyancy * (next_z - pressure)
        vx_bx = vx_bx - step_ratio * b_bx * (pressure[0:1] - p_bx)
        vy_by = vy_by - step_ratio * b_by * (pressure[:, 0:1] - p_by)
        lower_x = jnp.where(has_below_x, vx_bx, 0.0)
        lower_y = jnp.where(has_below_y, vy_by, 0.0)
        prev_x = jnp.concatenate([lower_x, vel_x[:-1]], 0)
        prev_y = jnp.concatenate([lower_y, vel_y[:, :-1]], 1)
        prev_z = jnp.concatenate([z_edge, vel_z[:, :, :-1]], 2)
        divergence = vel_x - prev_x + (vel_y - prev_y) + (vel_z - prev_z)
        pressure = pressure + step_ratio * stiffness * (
            source[:, :, step, :] + forcing - divergence
        )
        if step + 1 < steps:
            above_x = from_behind(pressure[0:1], "gx", -1)
            above_y = y_plane_from_behind(pressure[:, 0], "gy", -1)
            p_bx = from_behind(pressure[-1:], "gx", 1)
            p_by = y_plane_from_behind(pressure[:, -1], "gy", 1)
    return (pressure, vel_x, vel_y, vel_z)


def solution(mesh):
    in_specs = (
        P("gx", "gy", None),
        P("gx", "gy", None),
        P("gx", "gy", None),
        P("gx", "gy", None),
        P("gx", "gy", None),
        P(("gx", "gy"), None, None),
        P(("gx", "gy"), None),
        P(("gx", "gy")),
        P("gx", "gy", None),
        P(),
    )
    out_specs = (P("gx", "gy", None), P("gx", "gy", None), P("gx", "gy", None), P("gx", "gy", None))
    return jax.shard_map(body, mesh=mesh, in_specs=in_specs, out_specs=out_specs, check_vma=False)
```

```python
import jax
import jax.numpy as jnp
from jax import lax
from jax.sharding import PartitionSpec as P

step_ratio = 0.4
gas_density = 0.001
gas_stiffness = 5.29e-05


def from_behind(block, axis, distance):
    devices = range(lax.axis_size(axis))
    route = [(i - distance, i) for i in devices if i - distance in devices]
    return lax.ppermute(block, axis, route)


def y_plane_from_behind(plane, axis, distance):
    return from_behind(plane, axis, distance)[:, None, :]


def material(void_frac):
    liquid = 1.0 - void_frac
    buoyancy = 1.0 / (liquid + void_frac * gas_density)
    stiffness = 1.0 / (liquid + void_frac / gas_stiffness)
    return (buoyancy, stiffness)


def bubble_source(waves, bubble_dest, bubble_column, cells, ready):
    tiles_x = lax.axis_size("gx")
    tiles_y = lax.axis_size("gy")
    devices = tiles_x * tiles_y
    bubbles = waves.shape[0]
    steps = waves.shape[1]
    depth = waves.shape[2]
    capacity = 2 * bubbles // devices
    slots = devices * capacity
    dest = bubble_dest[:, 0]
    owners = (dest[:, None] == jnp.arange(devices, dtype=jnp.int32)[None, :]).astype(jnp.int32)
    rank = jnp.sum(jnp.cumsum(owners, axis=0) * owners, axis=1) - 1
    slot_ids = dest * capacity + rank
    placed = slot_ids[None, :] == jnp.arange(slots, dtype=jnp.int32)[:, None]
    outgoing = jnp.dot(
        placed.astype(jnp.bfloat16),
        waves.reshape(bubbles, steps * depth),
        preferred_element_type=jnp.float32,
    ).astype(jnp.bfloat16)
    out_cols = jnp.max(jnp.where(placed, bubble_column[None, :] + 1, 0), axis=1) - 1
    in_cols = lax.all_to_all(
        out_cols.reshape(devices, capacity),
        ("gx", "gy"),
        split_axis=0,
        concat_axis=0,
        tiled=True,
    )
    in_cols, outgoing, ready = lax.optimization_barrier((in_cols, outgoing, ready))
    incoming = lax.all_to_all(
        outgoing.reshape(devices, capacity, steps * depth),
        ("gx", "gy"),
        split_axis=0,
        concat_axis=0,
        tiled=True,
    )
    hits = (
        jnp.arange(cells, dtype=jnp.int32)[:, None] == in_cols.reshape(slots)[None, :]
    ).astype(jnp.bfloat16)
    source = jnp.dot(
        hits, incoming.reshape(slots, steps * depth), preferred_element_type=jnp.float32
    )
    return source, incoming, ready


def incident_plane(history, delays, size_y, depth):
    tiles_x = lax.axis_size("gx")
    my_tile = lax.axis_index("gx")
    cycle = jnp.arange(tiles_x, dtype=jnp.int32)
    dist = jnp.abs(cycle - my_tile)
    dist = jnp.minimum(dist, tiles_x - dist)
    weight = 1.0 / (1.0 + 2.0 * dist.astype(jnp.float32) / tiles_x)
    wanted = lax.dynamic_index_in_dim(delays, my_tile, 1, keepdims=False)
    chosen = jnp.take(history, wanted, axis=0)
    rows = lax.all_to_all(chosen, "gx", split_axis=0, concat_axis=0, tiled=True)
    return jnp.sum(weight[:, None, None] * rows.astype(jnp.float32), axis=0)


def body(
    pressure, vel_x, vel_y, vel_z, void_frac, waves, bubble_dest, bubble_column, history, delays
):
    size_x, size_y, depth = pressure.shape
    steps = waves.shape[1]
    ix = lax.axis_index("gx")
    iy = lax.axis_index("gy")
    has_below_x = ix > 0
    has_below_y = iy > 0
    buoyancy, stiffness = material(void_frac)

    above_x = from_behind(pressure[0:1], "gx", -1)
    above_y = y_plane_from_behind(pressure[:, 0], "gy", -1)
    below_x = from_behind(
        jnp.concatenate([pressure[-1:], vel_x[-1:], void_frac[-1:]], 0), "gx", 1
    )
    below_y = from_behind(
        jnp.stack([pressure[:, -1], vel_y[:, -1], void_frac[:, -1]], 0), "gy", 1
    )
    below_y = jnp.moveaxis(below_y, 0, 1)

    ready = (above_x, above_y, below_x, below_y)
    source, incoming, ready = bubble_source(
        waves, bubble_dest, bubble_column, size_x * size_y, ready
    )
    above_x, above_y, below_x, below_y = ready
    history, _ = lax.optimization_barrier((history, incoming))
    incident = incident_plane(history, delays, size_y, depth)
    source = source.reshape(size_x, size_y, steps, depth)
    p_bx, vx_bx, void_bx = below_x[0:1], below_x[1:2], below_x[2:3]
    p_by, vy_by, void_by = below_y[:, 0:1], below_y[:, 1:2], below_y[:, 2:3]
    b_bx, _ = material(void_bx)
    b_by, _ = material(void_by)
    forcing = jnp.zeros_like(pressure).at[0].set(incident)
    z_edge = jnp.zeros((size_x, size_y, 1), jnp.float32)

    for step in range(steps):
        next_x = jnp.concatenate([pressure[1:], above_x], 0)
        next_y = jnp.concatenate([pressure[:, 1:], above_y], 1)
        next_z = jnp.concatenate([pressure[:, :, 1:], z_edge], 2)
        vel_x = vel_x - step_ratio * buoyancy * (next_x - pressure)
        vel_y = vel_y - step_ratio * buoyancy * (next_y - pressure)
        vel_z = vel_z - step_ratio * buoyancy * (next_z - pressure)
        vx_bx = vx_bx - step_ratio * b_bx * (pressure[0:1] - p_bx)
        vy_by = vy_by - step_ratio * b_by * (pressure[:, 0:1] - p_by)
        lower_x = jnp.where(has_below_x, vx_bx, 0.0)
        lower_y = jnp.where(has_below_y, vy_by, 0.0)
        prev_x = jnp.concatenate([lower_x, vel_x[:-1]], 0)
        prev_y = jnp.concatenate([lower_y, vel_y[:, :-1]], 1)
        prev_z = jnp.concatenate([z_edge, vel_z[:, :, :-1]], 2)
        divergence = vel_x - prev_x + (vel_y - prev_y) + (vel_z - prev_z)
        if step + 1 < steps:
            divergence = lax.optimization_barrier(divergence)
        pressure = pressure + step_ratio * stiffness * (
            source[:, :, step, :] - divergence + forcing
        )
        if step + 1 < steps:
            above_x = from_behind(pressure[0:1], "gx", -1)
            above_y = y_plane_from_behind(pressure[:, 0], "gy", -1)
            p_bx = from_behind(pressure[-1:], "gx", 1)
            p_by = y_plane_from_behind(pressure[:, -1], "gy", 1)
    return (pressure, vel_x, vel_y, vel_z)


def solution(mesh):
    in_specs = (
        P("gx", "gy", None),
        P("gx", "gy", None),
        P("gx", "gy", None),
        P("gx", "gy", None),
        P("gx", "gy", None),
        P(("gx", "gy"), None, None),
        P(("gx", "gy"), None),
        P(("gx", "gy")),
        P("gx", "gy", None),
        P(),
    )
    out_specs = (P("gx", "gy", None), P("gx", "gy", None), P("gx", "gy", None), P("gx", "gy", None))
    return jax.shard_map(body, mesh=mesh, in_specs=in_specs, out_specs=out_specs, check_vma=False)
```

```python
import jax
import jax.numpy as jnp
from jax import lax
from jax.sharding import PartitionSpec as P

step_ratio = 0.4
gas_density = 0.001
gas_stiffness = 5.29e-05


def from_behind(block, axis, distance):
    devices = range(lax.axis_size(axis))
    route = [(i - distance, i) for i in devices if i - distance in devices]
    return lax.ppermute(block, axis, route)


def y_plane_from_behind(plane, axis, distance):
    return from_behind(plane, axis, distance)[:, None, :]


def material(void_frac):
    liquid = 1.0 - void_frac
    buoyancy = 1.0 / (liquid + void_frac * gas_density)
    stiffness = 1.0 / (liquid + void_frac / gas_stiffness)
    return (buoyancy, stiffness)


def bubble_source(waves, bubble_dest, bubble_column, cells, ready):
    tiles_x = lax.axis_size("gx")
    tiles_y = lax.axis_size("gy")
    devices = tiles_x * tiles_y
    bubbles = waves.shape[0]
    steps = waves.shape[1]
    depth = waves.shape[2]
    capacity = 2 * bubbles // devices
    slots = devices * capacity
    dest = bubble_dest[:, 0]
    owners = (dest[:, None] == jnp.arange(devices, dtype=jnp.int32)[None, :]).astype(jnp.int32)
    rank = jnp.sum(jnp.cumsum(owners, axis=0) * owners, axis=1) - 1
    slot_ids = dest * capacity + rank
    placed = slot_ids[None, :] == jnp.arange(slots, dtype=jnp.int32)[:, None]
    outgoing = jnp.dot(
        placed.astype(jnp.bfloat16),
        waves.reshape(bubbles, steps * depth),
        preferred_element_type=jnp.float32,
    ).astype(jnp.bfloat16)
    out_cols = jnp.max(jnp.where(placed, bubble_column[None, :] + 1, 0), axis=1) - 1
    outgoing, ready = lax.optimization_barrier((outgoing, ready))
    incoming = lax.all_to_all(
        outgoing.reshape(devices, capacity, steps * depth),
        ("gx", "gy"),
        split_axis=0,
        concat_axis=0,
        tiled=True,
    )
    out_cols, incoming = lax.optimization_barrier((out_cols, incoming))
    in_cols = lax.all_to_all(
        out_cols.reshape(devices, capacity),
        ("gx", "gy"),
        split_axis=0,
        concat_axis=0,
        tiled=True,
    )
    hits = (
        jnp.arange(cells, dtype=jnp.int32)[:, None] == in_cols.reshape(slots)[None, :]
    ).astype(jnp.bfloat16)
    source = jnp.dot(
        hits, incoming.reshape(slots, steps * depth), preferred_element_type=jnp.float32
    )
    return source, incoming, ready


def incident_plane(history, delays, after):
    tiles_x = lax.axis_size("gx")
    my_tile = lax.axis_index("gx")
    cycle = jnp.arange(tiles_x, dtype=jnp.int32)
    dist = jnp.abs(cycle - my_tile)
    dist = jnp.minimum(dist, tiles_x - dist)
    weight = 1.0 / (1.0 + 2.0 * dist.astype(jnp.float32) / tiles_x)
    wanted = lax.dynamic_index_in_dim(delays, my_tile, 1, keepdims=False)
    chosen = jnp.take(history, wanted, axis=0)
    chosen, _ = lax.optimization_barrier((chosen, after))
    rows = lax.all_to_all(chosen, "gx", split_axis=0, concat_axis=0, tiled=True)
    return jnp.sum(weight[:, None, None] * rows.astype(jnp.float32), axis=0)


def body(
    pressure, vel_x, vel_y, vel_z, void_frac, waves, bubble_dest, bubble_column, history, delays
):
    size_x, size_y, depth = pressure.shape
    steps = waves.shape[1]
    ix = lax.axis_index("gx")
    iy = lax.axis_index("gy")
    has_below_x = ix > 0
    has_below_y = iy > 0
    buoyancy, stiffness = material(void_frac)

    above_x = from_behind(pressure[0:1], "gx", -1)
    above_y = y_plane_from_behind(pressure[:, 0], "gy", -1)
    below_x = from_behind(
        jnp.concatenate([pressure[-1:], vel_x[-1:], void_frac[-1:]], 0), "gx", 1
    )
    below_y = from_behind(
        jnp.stack([pressure[:, -1], vel_y[:, -1], void_frac[:, -1]], 0), "gy", 1
    )
    below_y = jnp.moveaxis(below_y, 0, 1)

    ready = (above_x, above_y, below_x, below_y)
    source, incoming, ready = bubble_source(
        waves, bubble_dest, bubble_column, size_x * size_y, ready
    )
    above_x, above_y, below_x, below_y = ready
    incident = incident_plane(history, delays, incoming)
    source = source.reshape(size_x, size_y, steps, depth)
    p_bx, vx_bx, void_bx = below_x[0:1], below_x[1:2], below_x[2:3]
    p_by, vy_by, void_by = below_y[:, 0:1], below_y[:, 1:2], below_y[:, 2:3]
    b_bx, _ = material(void_bx)
    b_by, _ = material(void_by)
    forcing = jnp.zeros_like(pressure).at[0].set(incident)
    z_edge = jnp.zeros((size_x, size_y, 1), jnp.float32)

    for step in range(steps):
        next_x = jnp.concatenate([pressure[1:], above_x], 0)
        next_y = jnp.concatenate([pressure[:, 1:], above_y], 1)
        next_z = jnp.concatenate([pressure[:, :, 1:], z_edge], 2)
        vel_x = vel_x - step_ratio * buoyancy * (next_x - pressure)
        vel_y = vel_y - step_ratio * buoyancy * (next_y - pressure)
        vel_z = vel_z - step_ratio * buoyancy * (next_z - pressure)
        vx_bx = vx_bx - step_ratio * b_bx * (pressure[0:1] - p_bx)
        vy_by = vy_by - step_ratio * b_by * (pressure[:, 0:1] - p_by)
        lower_x = jnp.where(has_below_x, vx_bx, 0.0)
        lower_y = jnp.where(has_below_y, vy_by, 0.0)
        prev_x = jnp.concatenate([lower_x, vel_x[:-1]], 0)
        prev_y = jnp.concatenate([lower_y, vel_y[:, :-1]], 1)
        prev_z = jnp.concatenate([z_edge, vel_z[:, :, :-1]], 2)
        divergence = vel_x - prev_x + (vel_y - prev_y) + (vel_z - prev_z)
        if step + 1 < steps:
            divergence = lax.optimization_barrier(divergence)
        pressure = pressure + step_ratio * stiffness * (
            source[:, :, step, :] - divergence + forcing
        )
        if step + 1 < steps:
            above_x = from_behind(pressure[0:1], "gx", -1)
            above_y = y_plane_from_behind(pressure[:, 0], "gy", -1)
            p_bx = from_behind(pressure[-1:], "gx", 1)
            p_by = y_plane_from_behind(pressure[:, -1], "gy", 1)
    return (pressure, vel_x, vel_y, vel_z)


def solution(mesh):
    in_specs = (
        P("gx", "gy", None),
        P("gx", "gy", None),
        P("gx", "gy", None),
        P("gx", "gy", None),
        P("gx", "gy", None),
        P(("gx", "gy"), None, None),
        P(("gx", "gy"), None),
        P(("gx", "gy")),
        P("gx", "gy", None),
        P(),
    )
    out_specs = (P("gx", "gy", None), P("gx", "gy", None), P("gx", "gy", None), P("gx", "gy", None))
    return jax.shard_map(body, mesh=mesh, in_specs=in_specs, out_specs=out_specs, check_vma=False)
```

```python
import jax
import jax.numpy as jnp
from jax import lax
from jax.sharding import PartitionSpec as P

step_ratio = 0.4
gas_density = 0.001
gas_stiffness = 5.29e-05


def from_behind(block, axis, distance):
    devices = range(lax.axis_size(axis))
    route = [(i - distance, i) for i in devices if i - distance in devices]
    return lax.ppermute(block, axis, route)


def y_plane_from_behind(plane, axis, distance):
    return from_behind(plane, axis, distance)[:, None, :]


def material(void_frac):
    liquid = 1.0 - void_frac
    buoyancy = 1.0 / (liquid + void_frac * gas_density)
    stiffness = 1.0 / (liquid + void_frac / gas_stiffness)
    return (buoyancy, stiffness)


def bubble_source(waves, bubble_dest, bubble_column, cells, ready):
    tiles_x = lax.axis_size("gx")
    tiles_y = lax.axis_size("gy")
    devices = tiles_x * tiles_y
    bubbles = waves.shape[0]
    steps = waves.shape[1]
    depth = waves.shape[2]
    capacity = 2 * bubbles // devices
    slots = devices * capacity
    dest = bubble_dest[:, 0]
    owners = (dest[:, None] == jnp.arange(devices, dtype=jnp.int32)[None, :]).astype(jnp.int32)
    rank = jnp.sum(jnp.cumsum(owners, axis=0) * owners, axis=1) - 1
    slot_ids = dest * capacity + rank
    placed = slot_ids[None, :] == jnp.arange(slots, dtype=jnp.int32)[:, None]
    outgoing = jnp.dot(
        placed.astype(jnp.bfloat16),
        waves.reshape(bubbles, steps * depth),
        preferred_element_type=jnp.float32,
    ).astype(jnp.bfloat16)
    out_cols = jnp.max(jnp.where(placed, bubble_column[None, :] + 1, 0), axis=1) - 1
    in_cols = lax.all_to_all(
        out_cols.reshape(devices, capacity),
        ("gx", "gy"),
        split_axis=0,
        concat_axis=0,
        tiled=True,
    )
    in_cols, outgoing, ready = lax.optimization_barrier((in_cols, outgoing, ready))
    incoming = lax.all_to_all(
        outgoing.reshape(devices, capacity, steps * depth),
        ("gx", "gy"),
        split_axis=0,
        concat_axis=0,
        tiled=True,
    )
    hits = (
        jnp.arange(cells, dtype=jnp.int32)[:, None] == in_cols.reshape(slots)[None, :]
    ).astype(jnp.bfloat16)
    source = jnp.dot(
        hits, incoming.reshape(slots, steps * depth), preferred_element_type=jnp.float32
    )
    return source, incoming, ready


def incident_plane(history, delays, after):
    tiles_x = lax.axis_size("gx")
    my_tile = lax.axis_index("gx")
    cycle = jnp.arange(tiles_x, dtype=jnp.int32)
    dist = jnp.abs(cycle - my_tile)
    dist = jnp.minimum(dist, tiles_x - dist)
    weight = 1.0 / (1.0 + 2.0 * dist.astype(jnp.float32) / tiles_x)
    wanted = lax.dynamic_index_in_dim(delays, my_tile, 1, keepdims=False)
    chosen = jnp.take(history, wanted, axis=0)
    chosen, _ = lax.optimization_barrier((chosen, after))
    rows = lax.all_to_all(chosen, "gx", split_axis=0, concat_axis=0, tiled=True)
    return jnp.sum(weight[:, None, None] * rows.astype(jnp.float32), axis=0)


def body(
    pressure, vel_x, vel_y, vel_z, void_frac, waves, bubble_dest, bubble_column, history, delays
):
    size_x, size_y, depth = pressure.shape
    steps = waves.shape[1]
    ix = lax.axis_index("gx")
    iy = lax.axis_index("gy")
    has_below_x = ix > 0
    has_below_y = iy > 0
    buoyancy, stiffness = material(void_frac)

    above_x = from_behind(pressure[0:1], "gx", -1)
    above_y = y_plane_from_behind(pressure[:, 0], "gy", -1)
    below_x = from_behind(
        jnp.concatenate([pressure[-1:], vel_x[-1:], void_frac[-1:]], 0), "gx", 1
    )
    below_y = from_behind(
        jnp.stack([pressure[:, -1], vel_y[:, -1], void_frac[:, -1]], 0), "gy", 1
    )
    below_y = jnp.moveaxis(below_y, 0, 1)

    ready = (above_x, above_y, below_x, below_y)
    source, incoming, ready = bubble_source(
        waves, bubble_dest, bubble_column, size_x * size_y, ready
    )
    above_x, above_y, below_x, below_y = ready
    incident = incident_plane(history, delays, incoming)
    source = source.reshape(size_x, size_y, steps, depth)
    p_bx, vx_bx, void_bx = below_x[0:1], below_x[1:2], below_x[2:3]
    p_by, vy_by, void_by = below_y[:, 0:1], below_y[:, 1:2], below_y[:, 2:3]
    b_bx, _ = material(void_bx)
    b_by, _ = material(void_by)
    forcing = jnp.zeros_like(pressure).at[0].set(incident)
    z_edge = jnp.zeros((size_x, size_y, 1), jnp.float32)

    for step in range(steps):
        next_x = jnp.concatenate([pressure[1:], above_x], 0)
        next_y = jnp.concatenate([pressure[:, 1:], above_y], 1)
        next_z = jnp.concatenate([pressure[:, :, 1:], z_edge], 2)
        vel_x = vel_x - step_ratio * buoyancy * (next_x - pressure)
        vel_y = vel_y - step_ratio * buoyancy * (next_y - pressure)
        vel_z = vel_z - step_ratio * buoyancy * (next_z - pressure)
        vx_bx = vx_bx - step_ratio * b_bx * (pressure[0:1] - p_bx)
        vy_by = vy_by - step_ratio * b_by * (pressure[:, 0:1] - p_by)
        lower_x = jnp.where(has_below_x, vx_bx, 0.0)
        lower_y = jnp.where(has_below_y, vy_by, 0.0)
        prev_x = jnp.concatenate([lower_x, vel_x[:-1]], 0)
        prev_y = jnp.concatenate([lower_y, vel_y[:, :-1]], 1)
        prev_z = jnp.concatenate([z_edge, vel_z[:, :, :-1]], 2)
        divergence = vel_x - prev_x + (vel_y - prev_y) + (vel_z - prev_z)
        if step + 1 < steps:
            divergence = lax.optimization_barrier(divergence)
        pressure = pressure + step_ratio * stiffness * (
            source[:, :, step, :] - divergence + forcing
        )
        if step + 1 < steps:
            above_x = from_behind(pressure[0:1], "gx", -1)
            above_y = y_plane_from_behind(pressure[:, 0], "gy", -1)
            p_bx = from_behind(pressure[-1:], "gx", 1)
            p_by = y_plane_from_behind(pressure[:, -1], "gy", 1)
    return (pressure, vel_x, vel_y, vel_z)


def solution(mesh):
    in_specs = (
        P("gx", "gy", None),
        P("gx", "gy", None),
        P("gx", "gy", None),
        P("gx", "gy", None),
        P("gx", "gy", None),
        P(("gx", "gy"), None, None),
        P(("gx", "gy"), None),
        P(("gx", "gy")),
        P("gx", "gy", None),
        P(),
    )
    out_specs = (P("gx", "gy", None), P("gx", "gy", None), P("gx", "gy", None), P("gx", "gy", None))
    return jax.shard_map(body, mesh=mesh, in_specs=in_specs, out_specs=out_specs, check_vma=False)
```

```python
import jax
import jax.numpy as jnp
from jax import lax
from jax.sharding import PartitionSpec as P

step_ratio = 0.4
gas_density = 0.001
gas_stiffness = 5.29e-05


def from_behind(block, axis, distance):
    devices = range(lax.axis_size(axis))
    route = [(i - distance, i) for i in devices if i - distance in devices]
    return lax.ppermute(block, axis, route)


def y_plane_from_behind(plane, axis, distance):
    return from_behind(plane, axis, distance)[:, None, :]


def material(void_frac):
    liquid = 1.0 - void_frac
    buoyancy = 1.0 / (liquid + void_frac * gas_density)
    stiffness = 1.0 / (liquid + void_frac / gas_stiffness)
    return (buoyancy, stiffness)


def bubble_source(waves, bubble_dest, bubble_column, cells, ready):
    tiles_x = lax.axis_size("gx")
    tiles_y = lax.axis_size("gy")
    devices = tiles_x * tiles_y
    bubbles = waves.shape[0]
    steps = waves.shape[1]
    depth = waves.shape[2]
    capacity = 2 * bubbles // devices
    slots = devices * capacity
    dest = bubble_dest[:, 0]
    owners = (dest[:, None] == jnp.arange(devices, dtype=jnp.int32)[None, :]).astype(jnp.bfloat16)
    listed = jnp.arange(bubbles, dtype=jnp.int32)
    earlier = (listed[:, None] > listed[None, :]).astype(jnp.bfloat16)
    before = jnp.dot(earlier, owners, preferred_element_type=jnp.float32)
    rank = jnp.sum(before * owners.astype(jnp.float32), axis=1).astype(jnp.int32)
    slot_ids = dest * capacity + rank
    placed = slot_ids[None, :] == jnp.arange(slots, dtype=jnp.int32)[:, None]
    outgoing = jnp.dot(
        placed.astype(jnp.bfloat16),
        waves.reshape(bubbles, steps * depth),
        preferred_element_type=jnp.float32,
    ).astype(jnp.bfloat16)
    out_cols = jnp.max(jnp.where(placed, bubble_column[None, :] + 1, 0), axis=1) - 1
    in_cols = lax.all_to_all(
        out_cols.reshape(devices, capacity),
        ("gx", "gy"),
        split_axis=0,
        concat_axis=0,
        tiled=True,
    )
    in_cols, outgoing, ready = lax.optimization_barrier((in_cols, outgoing, ready))
    incoming = lax.all_to_all(
        outgoing.reshape(devices, capacity, steps * depth),
        ("gx", "gy"),
        split_axis=0,
        concat_axis=0,
        tiled=True,
    )
    hits = (
        jnp.arange(cells, dtype=jnp.int32)[:, None] == in_cols.reshape(slots)[None, :]
    ).astype(jnp.bfloat16)
    source = jnp.dot(
        hits, incoming.reshape(slots, steps * depth), preferred_element_type=jnp.float32
    )
    return source, incoming, ready


def incident_plane(history, delays, after):
    tiles_x = lax.axis_size("gx")
    my_tile = lax.axis_index("gx")
    cycle = jnp.arange(tiles_x, dtype=jnp.int32)
    dist = jnp.abs(cycle - my_tile)
    dist = jnp.minimum(dist, tiles_x - dist)
    weight = 1.0 / (1.0 + 2.0 * dist.astype(jnp.float32) / tiles_x)
    wanted = lax.dynamic_index_in_dim(delays, my_tile, 1, keepdims=False)
    chosen = jnp.take(history, wanted, axis=0)
    chosen, _ = lax.optimization_barrier((chosen, after))
    rows = lax.all_to_all(chosen, "gx", split_axis=0, concat_axis=0, tiled=True)
    return jnp.sum(weight[:, None, None] * rows.astype(jnp.float32), axis=0)


def body(
    pressure, vel_x, vel_y, vel_z, void_frac, waves, bubble_dest, bubble_column, history, delays
):
    size_x, size_y, depth = pressure.shape
    steps = waves.shape[1]
    ix = lax.axis_index("gx")
    iy = lax.axis_index("gy")
    has_below_x = ix > 0
    has_below_y = iy > 0
    buoyancy, stiffness = material(void_frac)

    above_x = from_behind(pressure[0:1], "gx", -1)
    above_y = y_plane_from_behind(pressure[:, 0], "gy", -1)
    below_x = from_behind(
        jnp.concatenate([pressure[-1:], vel_x[-1:], void_frac[-1:]], 0), "gx", 1
    )
    below_y = from_behind(
        jnp.stack([pressure[:, -1], vel_y[:, -1], void_frac[:, -1]], 0), "gy", 1
    )
    below_y = jnp.moveaxis(below_y, 0, 1)

    ready = (above_x, above_y, below_x, below_y)
    source, incoming, ready = bubble_source(
        waves, bubble_dest, bubble_column, size_x * size_y, ready
    )
    above_x, above_y, below_x, below_y = ready
    incident = incident_plane(history, delays, incoming)
    source = source.reshape(size_x, size_y, steps, depth)
    p_bx, vx_bx, void_bx = below_x[0:1], below_x[1:2], below_x[2:3]
    p_by, vy_by, void_by = below_y[:, 0:1], below_y[:, 1:2], below_y[:, 2:3]
    b_bx, _ = material(void_bx)
    b_by, _ = material(void_by)
    forcing = jnp.zeros_like(pressure).at[0].set(incident)
    z_edge = jnp.zeros((size_x, size_y, 1), jnp.float32)

    for step in range(steps):
        next_x = jnp.concatenate([pressure[1:], above_x], 0)
        next_y = jnp.concatenate([pressure[:, 1:], above_y], 1)
        next_z = jnp.concatenate([pressure[:, :, 1:], z_edge], 2)
        vel_x = vel_x - step_ratio * buoyancy * (next_x - pressure)
        vel_y = vel_y - step_ratio * buoyancy * (next_y - pressure)
        vel_z = vel_z - step_ratio * buoyancy * (next_z - pressure)
        vx_bx = vx_bx - step_ratio * b_bx * (pressure[0:1] - p_bx)
        vy_by = vy_by - step_ratio * b_by * (pressure[:, 0:1] - p_by)
        lower_x = jnp.where(has_below_x, vx_bx, 0.0)
        lower_y = jnp.where(has_below_y, vy_by, 0.0)
        prev_x = jnp.concatenate([lower_x, vel_x[:-1]], 0)
        prev_y = jnp.concatenate([lower_y, vel_y[:, :-1]], 1)
        prev_z = jnp.concatenate([z_edge, vel_z[:, :, :-1]], 2)
        divergence = vel_x - prev_x + (vel_y - prev_y) + (vel_z - prev_z)
        if step + 1 < steps:
            divergence = lax.optimization_barrier(divergence)
        pressure = pressure + step_ratio * stiffness * (
            source[:, :, step, :] - divergence + forcing
        )
        if step + 1 < steps:
            above_x = from_behind(pressure[0:1], "gx", -1)
            above_y = y_plane_from_behind(pressure[:, 0], "gy", -1)
            p_bx = from_behind(pressure[-1:], "gx", 1)
            p_by = y_plane_from_behind(pressure[:, -1], "gy", 1)
    return (pressure, vel_x, vel_y, vel_z)


def solution(mesh):
    in_specs = (
        P("gx", "gy", None),
        P("gx", "gy", None),
        P("gx", "gy", None),
        P("gx", "gy", None),
        P("gx", "gy", None),
        P(("gx", "gy"), None, None),
        P(("gx", "gy"), None),
        P(("gx", "gy")),
        P("gx", "gy", None),
        P(),
    )
    out_specs = (P("gx", "gy", None), P("gx", "gy", None), P("gx", "gy", None), P("gx", "gy", None))
    return jax.shard_map(body, mesh=mesh, in_specs=in_specs, out_specs=out_specs, check_vma=False)
```

```python
import jax
import jax.numpy as jnp
from jax import lax
from jax.sharding import PartitionSpec as P

step_ratio = 0.4
gas_density = 0.001
gas_stiffness = 5.29e-05


def from_behind(block, axis, distance):
    devices = range(lax.axis_size(axis))
    route = [(i - distance, i) for i in devices if i - distance in devices]
    return lax.ppermute(block, axis, route)


def y_plane_from_behind(plane, axis, distance):
    return from_behind(plane, axis, distance)[:, None, :]


def material(void_frac):
    liquid = 1.0 - void_frac
    buoyancy = 1.0 / (liquid + void_frac * gas_density)
    stiffness = 1.0 / (liquid + void_frac / gas_stiffness)
    return (buoyancy, stiffness)


def bubble_source(waves, bubble_dest, bubble_column, cells, ready):
    tiles_x = lax.axis_size("gx")
    tiles_y = lax.axis_size("gy")
    devices = tiles_x * tiles_y
    bubbles = waves.shape[0]
    steps = waves.shape[1]
    depth = waves.shape[2]
    capacity = 2 * bubbles // devices
    slots = devices * capacity
    dest = bubble_dest[:, 0]
    owners = (dest[:, None] == jnp.arange(devices, dtype=jnp.int32)[None, :]).astype(jnp.bfloat16)
    listed = jnp.arange(bubbles, dtype=jnp.int32)
    earlier = (listed[:, None] > listed[None, :]).astype(jnp.bfloat16)
    before = jnp.dot(earlier, owners, preferred_element_type=jnp.float32)
    rank = jnp.sum(before * owners.astype(jnp.float32), axis=1).astype(jnp.int32)
    slot_ids = dest * capacity + rank
    placed = slot_ids[None, :] == jnp.arange(slots, dtype=jnp.int32)[:, None]
    outgoing = jnp.dot(
        placed.astype(jnp.bfloat16),
        waves.reshape(bubbles, steps * depth),
        preferred_element_type=jnp.float32,
    ).astype(jnp.bfloat16)
    out_cols = jnp.max(jnp.where(placed, bubble_column[None, :], -1), axis=1)
    in_cols = lax.all_to_all(
        out_cols.reshape(devices, capacity),
        ("gx", "gy"),
        split_axis=0,
        concat_axis=0,
        tiled=True,
    )
    in_cols, outgoing, ready = lax.optimization_barrier((in_cols, outgoing, ready))
    incoming = lax.all_to_all(
        outgoing.reshape(devices, capacity, steps * depth),
        ("gx", "gy"),
        split_axis=0,
        concat_axis=0,
        tiled=True,
    )
    hits = (
        jnp.arange(cells, dtype=jnp.int32)[:, None] == in_cols.reshape(slots)[None, :]
    ).astype(jnp.bfloat16)
    source = jnp.dot(
        hits, incoming.reshape(slots, steps * depth), preferred_element_type=jnp.float32
    )
    return source, incoming, ready


def incident_plane(history, delays, after):
    tiles_x = lax.axis_size("gx")
    my_tile = lax.axis_index("gx")
    cycle = jnp.arange(tiles_x, dtype=jnp.int32)
    dist = jnp.abs(cycle - my_tile)
    dist = jnp.minimum(dist, tiles_x - dist)
    weight = 1.0 / (1.0 + 2.0 * dist.astype(jnp.float32) / tiles_x)
    wanted = lax.dynamic_index_in_dim(delays, my_tile, 1, keepdims=False)
    chosen = jnp.take(history, wanted, axis=0)
    chosen, _ = lax.optimization_barrier((chosen, after))
    rows = lax.all_to_all(chosen, "gx", split_axis=0, concat_axis=0, tiled=True)
    return jnp.sum(weight[:, None, None] * rows.astype(jnp.float32), axis=0)


def body(
    pressure, vel_x, vel_y, vel_z, void_frac, waves, bubble_dest, bubble_column, history, delays
):
    size_x, size_y, depth = pressure.shape
    steps = waves.shape[1]
    ix = lax.axis_index("gx")
    iy = lax.axis_index("gy")
    has_below_x = ix > 0
    has_below_y = iy > 0
    buoyancy, stiffness = material(void_frac)

    above_x = from_behind(pressure[0:1], "gx", -1)
    above_y = y_plane_from_behind(pressure[:, 0], "gy", -1)
    below_x = from_behind(
        jnp.concatenate([pressure[-1:], vel_x[-1:], void_frac[-1:]], 0), "gx", 1
    )
    below_y = from_behind(
        jnp.stack([pressure[:, -1], vel_y[:, -1], void_frac[:, -1]], 0), "gy", 1
    )
    below_y = jnp.moveaxis(below_y, 0, 1)

    ready = (above_x, above_y, below_x, below_y)
    source, incoming, ready = bubble_source(
        waves, bubble_dest, bubble_column, size_x * size_y, ready
    )
    above_x, above_y, below_x, below_y = ready
    incident = incident_plane(history, delays, incoming)
    source = source.reshape(size_x, size_y, steps, depth)
    p_bx, vx_bx, void_bx = below_x[0:1], below_x[1:2], below_x[2:3]
    p_by, vy_by, void_by = below_y[:, 0:1], below_y[:, 1:2], below_y[:, 2:3]
    b_bx, _ = material(void_bx)
    b_by, _ = material(void_by)
    forcing = jnp.zeros_like(pressure).at[0].set(incident)
    z_edge = jnp.zeros((size_x, size_y, 1), jnp.float32)

    for step in range(steps):
        next_x = jnp.concatenate([pressure[1:], above_x], 0)
        next_y = jnp.concatenate([pressure[:, 1:], above_y], 1)
        next_z = jnp.concatenate([pressure[:, :, 1:], z_edge], 2)
        vel_x = vel_x - step_ratio * buoyancy * (next_x - pressure)
        vel_y = vel_y - step_ratio * buoyancy * (next_y - pressure)
        vel_z = vel_z - step_ratio * buoyancy * (next_z - pressure)
        vx_bx = vx_bx - step_ratio * b_bx * (pressure[0:1] - p_bx)
        vy_by = vy_by - step_ratio * b_by * (pressure[:, 0:1] - p_by)
        lower_x = jnp.where(has_below_x, vx_bx, 0.0)
        lower_y = jnp.where(has_below_y, vy_by, 0.0)
        prev_x = jnp.concatenate([lower_x, vel_x[:-1]], 0)
        prev_y = jnp.concatenate([lower_y, vel_y[:, :-1]], 1)
        prev_z = jnp.concatenate([z_edge, vel_z[:, :, :-1]], 2)
        divergence = vel_x - prev_x + (vel_y - prev_y) + (vel_z - prev_z)
        if step + 1 < steps:
            divergence = lax.optimization_barrier(divergence)
        pressure = pressure + step_ratio * stiffness * (
            source[:, :, step, :] - divergence + forcing
        )
        if step + 1 < steps:
            above_x = from_behind(pressure[0:1], "gx", -1)
            above_y = y_plane_from_behind(pressure[:, 0], "gy", -1)
            p_bx = from_behind(pressure[-1:], "gx", 1)
            p_by = y_plane_from_behind(pressure[:, -1], "gy", 1)
    return (pressure, vel_x, vel_y, vel_z)


def solution(mesh):
    in_specs = (
        P("gx", "gy", None),
        P("gx", "gy", None),
        P("gx", "gy", None),
        P("gx", "gy", None),
        P("gx", "gy", None),
        P(("gx", "gy"), None, None),
        P(("gx", "gy"), None),
        P(("gx", "gy")),
        P("gx", "gy", None),
        P(),
    )
    out_specs = (P("gx", "gy", None), P("gx", "gy", None), P("gx", "gy", None), P("gx", "gy", None))
    return jax.shard_map(body, mesh=mesh, in_specs=in_specs, out_specs=out_specs, check_vma=False)
```

```python
import jax
import jax.numpy as jnp
from jax import lax
from jax.sharding import PartitionSpec as P

step_ratio = 0.4
gas_density = 0.001
gas_stiffness = 5.29e-05


def from_behind(block, axis, distance):
    devices = range(lax.axis_size(axis))
    route = [(i - distance, i) for i in devices if i - distance in devices]
    return lax.ppermute(block, axis, route)


def y_plane_from_behind(plane, axis, distance):
    return from_behind(plane, axis, distance)[:, None, :]


def material(void_frac):
    liquid = 1.0 - void_frac
    buoyancy = 1.0 / (liquid + void_frac * gas_density)
    stiffness = 1.0 / (liquid + void_frac / gas_stiffness)
    return (buoyancy, stiffness)


def bubble_source(waves, bubble_dest, bubble_column, cells, ready):
    tiles_x = lax.axis_size("gx")
    tiles_y = lax.axis_size("gy")
    devices = tiles_x * tiles_y
    bubbles = waves.shape[0]
    steps = waves.shape[1]
    depth = waves.shape[2]
    capacity = 2 * bubbles // devices
    slots = devices * capacity
    dest = bubble_dest[:, 0]
    owners = (dest[:, None] == jnp.arange(devices, dtype=jnp.int32)[None, :]).astype(jnp.bfloat16)
    listed = jnp.arange(bubbles, dtype=jnp.int32)
    earlier = (listed[:, None] > listed[None, :]).astype(jnp.bfloat16)
    before = jnp.dot(earlier, owners, preferred_element_type=jnp.float32)
    rank = jnp.sum(before * owners.astype(jnp.float32), axis=1).astype(jnp.int32)
    slot_ids = dest * capacity + rank
    placed = slot_ids[None, :] == jnp.arange(slots, dtype=jnp.int32)[:, None]
    outgoing = jnp.dot(
        placed.astype(jnp.bfloat16),
        waves.reshape(bubbles, steps * depth),
        preferred_element_type=jnp.float32,
    ).astype(jnp.bfloat16)
    out_cols = jnp.max(jnp.where(placed, bubble_column[None, :] + 1, 0), axis=1) - 1
    in_cols = lax.all_to_all(
        out_cols.reshape(devices, capacity),
        ("gx", "gy"),
        split_axis=0,
        concat_axis=0,
        tiled=True,
    )
    in_cols, outgoing, ready = lax.optimization_barrier((in_cols, outgoing, ready))
    incoming = lax.all_to_all(
        outgoing.reshape(devices, capacity, steps * depth),
        ("gx", "gy"),
        split_axis=0,
        concat_axis=0,
        tiled=True,
    )
    hits = (
        jnp.arange(cells, dtype=jnp.int32)[:, None] == in_cols.reshape(slots)[None, :]
    ).astype(jnp.bfloat16)
    source = jnp.dot(
        hits, incoming.reshape(slots, steps * depth), preferred_element_type=jnp.float32
    )
    return source, incoming, ready


def incident_plane(history, delays, after):
    tiles_x = lax.axis_size("gx")
    my_tile = lax.axis_index("gx")
    cycle = jnp.arange(tiles_x, dtype=jnp.int32)
    dist = jnp.abs(cycle - my_tile)
    dist = jnp.minimum(dist, tiles_x - dist)
    weight = 1.0 / (1.0 + 2.0 * dist.astype(jnp.float32) / tiles_x)
    wanted = lax.dynamic_index_in_dim(delays, my_tile, 1, keepdims=False)
    chosen = jnp.take(history, wanted, axis=0)
    chosen, _ = lax.optimization_barrier((chosen, after))
    rows = lax.all_to_all(chosen, "gx", split_axis=0, concat_axis=0, tiled=True)
    return jnp.sum(weight[:, None, None] * rows.astype(jnp.float32), axis=0)


def body(
    pressure, vel_x, vel_y, vel_z, void_frac, waves, bubble_dest, bubble_column, history, delays
):
    size_x, size_y, depth = pressure.shape
    steps = waves.shape[1]
    ix = lax.axis_index("gx")
    iy = lax.axis_index("gy")
    has_below_x = ix > 0
    has_below_y = iy > 0
    buoyancy, stiffness = material(void_frac)

    above_x = from_behind(pressure[0:1], "gx", -1)
    above_y = y_plane_from_behind(pressure[:, 0], "gy", -1)
    kick_x = step_ratio * buoyancy[-1:]
    kick_y = step_ratio * buoyancy[:, -1]
    below_x = from_behind(
        jnp.concatenate([vel_x[-1:] + kick_x * pressure[-1:], kick_x], 0), "gx", 1
    )
    below_y = from_behind(
        jnp.stack([vel_y[:, -1] + kick_y * pressure[:, -1], kick_y], 0), "gy", 1
    )
    below_y = jnp.moveaxis(below_y, 0, 1)

    ready = (above_x, above_y, below_x, below_y)
    source, incoming, ready = bubble_source(
        waves, bubble_dest, bubble_column, size_x * size_y, ready
    )
    above_x, above_y, below_x, below_y = ready
    incident = incident_plane(history, delays, incoming)
    source = source.reshape(size_x, size_y, steps, depth)
    lead_x, kick_bx = below_x[0:1], below_x[1:2]
    lead_y, kick_by = below_y[:, 0:1], below_y[:, 1:2]
    forcing = jnp.zeros_like(pressure).at[0].set(incident)
    z_edge = jnp.zeros((size_x, size_y, 1), jnp.float32)

    for step in range(steps):
        next_x = jnp.concatenate([pressure[1:], above_x], 0)
        next_y = jnp.concatenate([pressure[:, 1:], above_y], 1)
        next_z = jnp.concatenate([pressure[:, :, 1:], z_edge], 2)
        vel_x = vel_x - step_ratio * buoyancy * (next_x - pressure)
        vel_y = vel_y - step_ratio * buoyancy * (next_y - pressure)
        vel_z = vel_z - step_ratio * buoyancy * (next_z - pressure)
        if step == 0:
            vx_bx = lead_x - kick_bx * pressure[0:1]
            vy_by = lead_y - kick_by * pressure[:, 0:1]
        else:
            vx_bx = vx_bx - kick_bx * (pressure[0:1] - p_bx)
            vy_by = vy_by - kick_by * (pressure[:, 0:1] - p_by)
        lower_x = jnp.where(has_below_x, vx_bx, 0.0)
        lower_y = jnp.where(has_below_y, vy_by, 0.0)
        prev_x = jnp.concatenate([lower_x, vel_x[:-1]], 0)
        prev_y = jnp.concatenate([lower_y, vel_y[:, :-1]], 1)
        prev_z = jnp.concatenate([z_edge, vel_z[:, :, :-1]], 2)
        divergence = vel_x - prev_x + (vel_y - prev_y) + (vel_z - prev_z)
        if step + 1 < steps:
            divergence = lax.optimization_barrier(divergence)
        pressure = pressure + step_ratio * stiffness * (
            source[:, :, step, :] - divergence + forcing
        )
        if step + 1 < steps:
            above_x = from_behind(pressure[0:1], "gx", -1)
            above_y = y_plane_from_behind(pressure[:, 0], "gy", -1)
            p_bx = from_behind(pressure[-1:], "gx", 1)
            p_by = y_plane_from_behind(pressure[:, -1], "gy", 1)
    return (pressure, vel_x, vel_y, vel_z)


def solution(mesh):
    in_specs = (
        P("gx", "gy", None),
        P("gx", "gy", None),
        P("gx", "gy", None),
        P("gx", "gy", None),
        P("gx", "gy", None),
        P(("gx", "gy"), None, None),
        P(("gx", "gy"), None),
        P(("gx", "gy")),
        P("gx", "gy", None),
        P(),
    )
    out_specs = (P("gx", "gy", None), P("gx", "gy", None), P("gx", "gy", None), P("gx", "gy", None))
    return jax.shard_map(body, mesh=mesh, in_specs=in_specs, out_specs=out_specs, check_vma=False)
```

```python
import jax
import jax.numpy as jnp
from jax import lax
from jax.sharding import PartitionSpec as P

step_ratio = 0.4
gas_density = 0.001
gas_stiffness = 5.29e-05


def from_behind(block, axis, distance):
    devices = range(lax.axis_size(axis))
    route = [(i - distance, i) for i in devices if i - distance in devices]
    return lax.ppermute(block, axis, route)


def y_plane_from_behind(plane, axis, distance):
    return from_behind(plane, axis, distance)[:, None, :]


def material(void_frac):
    liquid = 1.0 - void_frac
    buoyancy = 1.0 / (liquid + void_frac * gas_density)
    stiffness = 1.0 / (liquid + void_frac / gas_stiffness)
    return (buoyancy, stiffness)


def bubble_source(waves, bubble_dest, bubble_column, cells, ready):
    tiles_x = lax.axis_size("gx")
    tiles_y = lax.axis_size("gy")
    devices = tiles_x * tiles_y
    bubbles = waves.shape[0]
    steps = waves.shape[1]
    depth = waves.shape[2]
    capacity = 2 * bubbles // devices
    slots = devices * capacity
    dest = bubble_dest[:, 0]
    owners = (dest[:, None] == jnp.arange(devices, dtype=jnp.int32)[None, :]).astype(jnp.bfloat16)
    listed = jnp.arange(bubbles, dtype=jnp.int32)
    earlier = (listed[:, None] > listed[None, :]).astype(jnp.bfloat16)
    before = jnp.dot(earlier, owners, preferred_element_type=jnp.float32)
    rank = jnp.sum(before * owners.astype(jnp.float32), axis=1).astype(jnp.int32)
    slot_ids = dest * capacity + rank
    placed = slot_ids[None, :] == jnp.arange(slots, dtype=jnp.int32)[:, None]
    outgoing = jnp.dot(
        placed.astype(jnp.bfloat16),
        waves.reshape(bubbles, steps * depth),
        preferred_element_type=jnp.float32,
    ).astype(jnp.bfloat16)
    out_cols = jnp.max(jnp.where(placed, bubble_column[None, :] + 1, 0), axis=1) - 1
    out_cols, ready = lax.optimization_barrier((out_cols, ready))
    in_cols = lax.all_to_all(
        out_cols.reshape(devices, capacity),
        ("gx", "gy"),
        split_axis=0,
        concat_axis=0,
        tiled=True,
    )
    in_cols, outgoing, ready = lax.optimization_barrier((in_cols, outgoing, ready))
    incoming = lax.all_to_all(
        outgoing.reshape(devices, capacity, steps * depth),
        ("gx", "gy"),
        split_axis=0,
        concat_axis=0,
        tiled=True,
    )
    hits = (
        jnp.arange(cells, dtype=jnp.int32)[:, None] == in_cols.reshape(slots)[None, :]
    ).astype(jnp.bfloat16)
    source = jnp.dot(
        hits, incoming.reshape(slots, steps * depth), preferred_element_type=jnp.float32
    )
    return source, incoming, ready


def incident_plane(history, delays, after):
    tiles_x = lax.axis_size("gx")
    my_tile = lax.axis_index("gx")
    cycle = jnp.arange(tiles_x, dtype=jnp.int32)
    dist = jnp.abs(cycle - my_tile)
    dist = jnp.minimum(dist, tiles_x - dist)
    weight = 1.0 / (1.0 + 2.0 * dist.astype(jnp.float32) / tiles_x)
    wanted = lax.dynamic_index_in_dim(delays, my_tile, 1, keepdims=False)
    chosen = jnp.take(history, wanted, axis=0)
    chosen, _ = lax.optimization_barrier((chosen, after))
    rows = lax.all_to_all(chosen, "gx", split_axis=0, concat_axis=0, tiled=True)
    return jnp.sum(weight[:, None, None] * rows.astype(jnp.float32), axis=0)


def body(
    pressure, vel_x, vel_y, vel_z, void_frac, waves, bubble_dest, bubble_column, history, delays
):
    size_x, size_y, depth = pressure.shape
    steps = waves.shape[1]
    ix = lax.axis_index("gx")
    iy = lax.axis_index("gy")
    has_below_x = ix > 0
    has_below_y = iy > 0
    buoyancy, stiffness = material(void_frac)

    above_x = from_behind(pressure[0:1], "gx", -1)
    above_y = y_plane_from_behind(pressure[:, 0], "gy", -1)
    below_x = from_behind(
        jnp.concatenate([pressure[-1:], vel_x[-1:], void_frac[-1:]], 0), "gx", 1
    )
    below_y = from_behind(
        jnp.stack([pressure[:, -1], vel_y[:, -1], void_frac[:, -1]], 0), "gy", 1
    )
    below_y = jnp.moveaxis(below_y, 0, 1)

    ready = (above_x, above_y, below_x, below_y)
    source, incoming, ready = bubble_source(
        waves, bubble_dest, bubble_column, size_x * size_y, ready
    )
    above_x, above_y, below_x, below_y = ready
    incident = incident_plane(history, delays, incoming)
    source = source.reshape(size_x, size_y, steps, depth)
    p_bx, vx_bx, void_bx = below_x[0:1], below_x[1:2], below_x[2:3]
    p_by, vy_by, void_by = below_y[:, 0:1], below_y[:, 1:2], below_y[:, 2:3]
    b_bx, _ = material(void_bx)
    b_by, _ = material(void_by)
    forcing = jnp.zeros_like(pressure).at[0].set(incident)
    z_edge = jnp.zeros((size_x, size_y, 1), jnp.float32)

    for step in range(steps):
        next_x = jnp.concatenate([pressure[1:], above_x], 0)
        next_y = jnp.concatenate([pressure[:, 1:], above_y], 1)
        next_z = jnp.concatenate([pressure[:, :, 1:], z_edge], 2)
        vel_x = vel_x - step_ratio * buoyancy * (next_x - pressure)
        vel_y = vel_y - step_ratio * buoyancy * (next_y - pressure)
        vel_z = vel_z - step_ratio * buoyancy * (next_z - pressure)
        vx_bx = vx_bx - step_ratio * b_bx * (pressure[0:1] - p_bx)
        vy_by = vy_by - step_ratio * b_by * (pressure[:, 0:1] - p_by)
        lower_x = jnp.where(has_below_x, vx_bx, 0.0)
        lower_y = jnp.where(has_below_y, vy_by, 0.0)
        prev_x = jnp.concatenate([lower_x, vel_x[:-1]], 0)
        prev_y = jnp.concatenate([lower_y, vel_y[:, :-1]], 1)
        prev_z = jnp.concatenate([z_edge, vel_z[:, :, :-1]], 2)
        divergence = vel_x - prev_x + (vel_y - prev_y) + (vel_z - prev_z)
        if step + 1 < steps:
            divergence = lax.optimization_barrier(divergence)
        pressure = pressure + step_ratio * stiffness * (
            source[:, :, step, :] - divergence + forcing
        )
        if step + 1 < steps:
            above_x = from_behind(pressure[0:1], "gx", -1)
            above_y = y_plane_from_behind(pressure[:, 0], "gy", -1)
            p_bx = from_behind(pressure[-1:], "gx", 1)
            p_by = y_plane_from_behind(pressure[:, -1], "gy", 1)
    return (pressure, vel_x, vel_y, vel_z)


def solution(mesh):
    in_specs = (
        P("gx", "gy", None),
        P("gx", "gy", None),
        P("gx", "gy", None),
        P("gx", "gy", None),
        P("gx", "gy", None),
        P(("gx", "gy"), None, None),
        P(("gx", "gy"), None),
        P(("gx", "gy")),
        P("gx", "gy", None),
        P(),
    )
    out_specs = (P("gx", "gy", None), P("gx", "gy", None), P("gx", "gy", None), P("gx", "gy", None))
    return jax.shard_map(body, mesh=mesh, in_specs=in_specs, out_specs=out_specs, check_vma=False)
```

```python
import jax
import jax.numpy as jnp
from jax import lax
from jax.sharding import PartitionSpec as P

step_ratio = 0.4
gas_density = 0.001
gas_stiffness = 5.29e-05


def from_behind(block, axis, distance):
    devices = range(lax.axis_size(axis))
    route = [(i - distance, i) for i in devices if i - distance in devices]
    return lax.ppermute(block, axis, route)


def y_plane_from_behind(plane, axis, distance):
    return from_behind(plane, axis, distance)[:, None, :]


def material(void_frac):
    liquid = 1.0 - void_frac
    buoyancy = 1.0 / (liquid + void_frac * gas_density)
    stiffness = 1.0 / (liquid + void_frac / gas_stiffness)
    return (buoyancy, stiffness)


def bubble_source(waves, bubble_dest, bubble_column, cells, ready):
    tiles_x = lax.axis_size("gx")
    tiles_y = lax.axis_size("gy")
    devices = tiles_x * tiles_y
    bubbles = waves.shape[0]
    steps = waves.shape[1]
    depth = waves.shape[2]
    capacity = 2 * bubbles // devices
    slots = devices * capacity
    dest = bubble_dest[:, 0]
    owners = (dest[:, None] == jnp.arange(devices, dtype=jnp.int32)[None, :]).astype(jnp.bfloat16)
    listed = jnp.arange(bubbles, dtype=jnp.int32)
    earlier = (listed[:, None] > listed[None, :]).astype(jnp.bfloat16)
    before = jnp.dot(earlier, owners, preferred_element_type=jnp.float32)
    rank = jnp.sum(before * owners.astype(jnp.float32), axis=1).astype(jnp.int32)
    slot_ids = dest * capacity + rank
    placed = slot_ids[None, :] == jnp.arange(slots, dtype=jnp.int32)[:, None]
    outgoing = jnp.dot(
        placed.astype(jnp.bfloat16),
        waves.reshape(bubbles, steps * depth),
        preferred_element_type=jnp.float32,
    ).astype(jnp.bfloat16)
    out_cols = jnp.max(jnp.where(placed, bubble_column[None, :] + 1, 0), axis=1) - 1
    in_cols = lax.all_to_all(
        out_cols.reshape(devices, capacity),
        ("gx", "gy"),
        split_axis=0,
        concat_axis=0,
        tiled=True,
    )
    in_cols, outgoing, ready = lax.optimization_barrier((in_cols, outgoing, ready))
    incoming = lax.all_to_all(
        outgoing.reshape(devices, capacity, steps * depth),
        ("gx", "gy"),
        split_axis=0,
        concat_axis=0,
        tiled=True,
    )
    hits = (
        jnp.arange(cells, dtype=jnp.int32)[:, None] == in_cols.reshape(slots)[None, :]
    ).astype(jnp.bfloat16)
    source = jnp.dot(
        hits, incoming.reshape(slots, steps * depth), preferred_element_type=jnp.float32
    )
    return source, incoming, ready


def incident_plane(history, delays, after):
    tiles_x = lax.axis_size("gx")
    my_tile = lax.axis_index("gx")
    cycle = jnp.arange(tiles_x, dtype=jnp.int32)
    dist = jnp.abs(cycle - my_tile)
    dist = jnp.minimum(dist, tiles_x - dist)
    weight = 1.0 / (1.0 + 2.0 * dist.astype(jnp.float32) / tiles_x)
    wanted = lax.dynamic_index_in_dim(delays, my_tile, 1, keepdims=False)
    chosen = jnp.take(history, wanted, axis=0)
    chosen, _ = lax.optimization_barrier((chosen, after))
    rows = lax.all_to_all(chosen, "gx", split_axis=0, concat_axis=0, tiled=True)
    return jnp.sum(weight[:, None, None] * rows.astype(jnp.float32), axis=0)


def body(
    pressure, vel_x, vel_y, vel_z, void_frac, waves, bubble_dest, bubble_column, history, delays
):
    size_x, size_y, depth = pressure.shape
    steps = waves.shape[1]
    ix = lax.axis_index("gx")
    iy = lax.axis_index("gy")
    has_below_x = ix > 0
    has_below_y = iy > 0
    buoyancy, stiffness = material(void_frac)

    above_x = from_behind(pressure[0:1], "gx", -1)
    above_y = y_plane_from_behind(pressure[:, 0], "gy", -1)
    below_x = from_behind(
        jnp.concatenate([pressure[-1:], vel_x[-1:], void_frac[-1:]], 0), "gx", 1
    )
    below_y = from_behind(
        jnp.stack([pressure[:, -1], vel_y[:, -1], void_frac[:, -1]], 0), "gy", 1
    )
    below_y = jnp.moveaxis(below_y, 0, 1)

    ready = (above_x, above_y, below_x, below_y)
    source, incoming, ready = bubble_source(
        waves, bubble_dest, bubble_column, size_x * size_y, ready
    )
    above_x, above_y, below_x, below_y = ready
    incident = incident_plane(history, delays, incoming)
    source = source.reshape(size_x, size_y, steps, depth)
    p_bx, vx_bx, void_bx = below_x[0:1], below_x[1:2], below_x[2:3]
    p_by, vy_by, void_by = below_y[:, 0:1], below_y[:, 1:2], below_y[:, 2:3]
    b_bx, _ = material(void_bx)
    b_by, _ = material(void_by)
    z_edge = jnp.zeros((size_x, size_y, 1), jnp.float32)

    for step in range(steps):
        next_x = jnp.concatenate([pressure[1:], above_x], 0)
        next_y = jnp.concatenate([pressure[:, 1:], above_y], 1)
        next_z = jnp.concatenate([pressure[:, :, 1:], z_edge], 2)
        vel_x = vel_x - step_ratio * buoyancy * (next_x - pressure)
        vel_y = vel_y - step_ratio * buoyancy * (next_y - pressure)
        vel_z = vel_z - step_ratio * buoyancy * (next_z - pressure)
        vx_bx = vx_bx - step_ratio * b_bx * (pressure[0:1] - p_bx)
        vy_by = vy_by - step_ratio * b_by * (pressure[:, 0:1] - p_by)
        lower_x = jnp.where(has_below_x, vx_bx, 0.0)
        lower_y = jnp.where(has_below_y, vy_by, 0.0)
        prev_x = jnp.concatenate([lower_x, vel_x[:-1]], 0)
        prev_y = jnp.concatenate([lower_y, vel_y[:, :-1]], 1)
        prev_z = jnp.concatenate([z_edge, vel_z[:, :, :-1]], 2)
        divergence = vel_x - prev_x + (vel_y - prev_y) + (vel_z - prev_z)
        if step + 1 < steps:
            divergence = lax.optimization_barrier(divergence)
        drive = source[:, :, step, :] - divergence
        first = pressure[0:1] + step_ratio * stiffness[0:1] * (drive[0:1] + incident[None])
        pressure = pressure + step_ratio * stiffness * drive
        pressure = lax.dynamic_update_slice_in_dim(pressure, first, 0, axis=0)
        if step + 1 < steps:
            above_x = from_behind(pressure[0:1], "gx", -1)
            above_y = y_plane_from_behind(pressure[:, 0], "gy", -1)
            p_bx = from_behind(pressure[-1:], "gx", 1)
            p_by = y_plane_from_behind(pressure[:, -1], "gy", 1)
    return (pressure, vel_x, vel_y, vel_z)


def solution(mesh):
    in_specs = (
        P("gx", "gy", None),
        P("gx", "gy", None),
        P("gx", "gy", None),
        P("gx", "gy", None),
        P("gx", "gy", None),
        P(("gx", "gy"), None, None),
        P(("gx", "gy"), None),
        P(("gx", "gy")),
        P("gx", "gy", None),
        P(),
    )
    out_specs = (P("gx", "gy", None), P("gx", "gy", None), P("gx", "gy", None), P("gx", "gy", None))
    return jax.shard_map(body, mesh=mesh, in_specs=in_specs, out_specs=out_specs, check_vma=False)
```

```python
import jax
import jax.numpy as jnp
from jax import lax
from jax.sharding import PartitionSpec as P

step_ratio = 0.4
gas_density = 0.001
gas_stiffness = 5.29e-05


def from_behind(block, axis, distance):
    devices = range(lax.axis_size(axis))
    route = [(i - distance, i) for i in devices if i - distance in devices]
    return lax.ppermute(block, axis, route)


def y_plane_from_behind(plane, axis, distance):
    return from_behind(plane, axis, distance)[:, None, :]


def material(void_frac):
    liquid = 1.0 - void_frac
    buoyancy = 1.0 / (liquid + void_frac * gas_density)
    stiffness = 1.0 / (liquid + void_frac / gas_stiffness)
    return (buoyancy, stiffness)


def bubble_source(waves, bubble_dest, bubble_column, cells, ready):
    tiles_x = lax.axis_size("gx")
    tiles_y = lax.axis_size("gy")
    devices = tiles_x * tiles_y
    bubbles = waves.shape[0]
    steps = waves.shape[1]
    depth = waves.shape[2]
    capacity = 2 * bubbles // devices
    slots = devices * capacity
    dest = bubble_dest[:, 0]
    owners = (dest[:, None] == jnp.arange(devices, dtype=jnp.int32)[None, :]).astype(jnp.bfloat16)
    listed = jnp.arange(bubbles, dtype=jnp.int32)
    earlier = (listed[:, None] > listed[None, :]).astype(jnp.bfloat16)
    before = jnp.dot(earlier, owners, preferred_element_type=jnp.float32)
    rank = jnp.sum(before * owners.astype(jnp.float32), axis=1).astype(jnp.int32)
    slot_ids = dest * capacity + rank
    placed = slot_ids[None, :] == jnp.arange(slots, dtype=jnp.int32)[:, None]
    outgoing = jnp.dot(
        placed.astype(jnp.bfloat16),
        waves.reshape(bubbles, steps * depth),
        preferred_element_type=jnp.float32,
    ).astype(jnp.bfloat16)
    out_cols = jnp.max(jnp.where(placed, bubble_column[None, :] + 1, 0), axis=1) - 1
    in_cols = lax.all_to_all(
        out_cols.reshape(devices, capacity),
        ("gx", "gy"),
        split_axis=0,
        concat_axis=0,
        tiled=True,
    )
    in_cols, outgoing, ready = lax.optimization_barrier((in_cols, outgoing, ready))
    incoming = lax.all_to_all(
        outgoing.reshape(devices, capacity, steps * depth),
        ("gx", "gy"),
        split_axis=0,
        concat_axis=0,
        tiled=True,
    )
    hits = (
        jnp.arange(cells, dtype=jnp.int32)[:, None] == in_cols.reshape(slots)[None, :]
    ).astype(jnp.bfloat16)
    source = jnp.dot(
        hits, incoming.reshape(slots, steps * depth), preferred_element_type=jnp.float32
    )
    return source, incoming, ready


def incident_plane(history, delays, after):
    tiles_x = lax.axis_size("gx")
    my_tile = lax.axis_index("gx")
    cycle = jnp.arange(tiles_x, dtype=jnp.int32)
    dist = jnp.abs(cycle - my_tile)
    dist = jnp.minimum(dist, tiles_x - dist)
    weight = 1.0 / (1.0 + 2.0 * dist.astype(jnp.float32) / tiles_x)
    wanted = lax.dynamic_index_in_dim(delays, my_tile, 1, keepdims=False)
    chosen = jnp.take(history, wanted, axis=0)
    chosen, _ = lax.optimization_barrier((chosen, after))
    rows = lax.all_to_all(chosen, "gx", split_axis=0, concat_axis=0, tiled=True)
    return jnp.sum(weight[:, None, None] * rows.astype(jnp.float32), axis=0)


def body(
    pressure, vel_x, vel_y, vel_z, void_frac, waves, bubble_dest, bubble_column, history, delays
):
    size_x, size_y, depth = pressure.shape
    steps = waves.shape[1]
    ix = lax.axis_index("gx")
    iy = lax.axis_index("gy")
    has_below_x = ix > 0
    has_below_y = iy > 0
    buoyancy, stiffness = material(void_frac)

    above_x = from_behind(pressure[0:1], "gx", -1)
    above_y = y_plane_from_behind(pressure[:, 0], "gy", -1)
    below_x = from_behind(
        jnp.concatenate([pressure[-1:], vel_x[-1:], void_frac[-1:]], 0), "gx", 1
    )
    below_y = from_behind(
        jnp.stack([pressure[:, -1], vel_y[:, -1], void_frac[:, -1]], 0), "gy", 1
    )
    below_y = jnp.moveaxis(below_y, 0, 1)

    ready = (above_x, above_y, below_x, below_y)
    source, incoming, ready = bubble_source(
        waves, bubble_dest, bubble_column, size_x * size_y, ready
    )
    above_x, above_y, below_x, below_y = ready
    incident = incident_plane(history, delays, incoming)
    source = source.reshape(size_x, size_y, steps, depth)
    p_bx, vx_bx, void_bx = below_x[0:1], below_x[1:2], below_x[2:3]
    p_by, vy_by, void_by = below_y[:, 0:1], below_y[:, 1:2], below_y[:, 2:3]
    b_bx, _ = material(void_bx)
    b_by, _ = material(void_by)
    z_edge = jnp.zeros((size_x, size_y, 1), jnp.float32)

    for step in range(steps):
        next_x = jnp.concatenate([pressure[1:], above_x], 0)
        next_y = jnp.concatenate([pressure[:, 1:], above_y], 1)
        next_z = jnp.concatenate([pressure[:, :, 1:], z_edge], 2)
        vel_x = vel_x - step_ratio * buoyancy * (next_x - pressure)
        vel_y = vel_y - step_ratio * buoyancy * (next_y - pressure)
        vel_z = vel_z - step_ratio * buoyancy * (next_z - pressure)
        vx_bx = vx_bx - step_ratio * b_bx * (pressure[0:1] - p_bx)
        vy_by = vy_by - step_ratio * b_by * (pressure[:, 0:1] - p_by)
        lower_x = jnp.where(has_below_x, vx_bx, 0.0)
        lower_y = jnp.where(has_below_y, vy_by, 0.0)
        prev_x = jnp.concatenate([lower_x, vel_x[:-1]], 0)
        prev_y = jnp.concatenate([lower_y, vel_y[:, :-1]], 1)
        prev_z = jnp.concatenate([z_edge, vel_z[:, :, :-1]], 2)
        divergence = vel_x - prev_x + (vel_y - prev_y) + (vel_z - prev_z)
        drive = source[:, :, step, :] - divergence
        first = pressure[0:1] + step_ratio * stiffness[0:1] * (drive[0:1] + incident[None])
        pressure = pressure + step_ratio * stiffness * drive
        pressure = lax.dynamic_update_slice_in_dim(pressure, first, 0, axis=0)
        if step + 1 < steps:
            above_x = from_behind(pressure[0:1], "gx", -1)
            above_y = y_plane_from_behind(pressure[:, 0], "gy", -1)
            p_bx = from_behind(pressure[-1:], "gx", 1)
            p_by = y_plane_from_behind(pressure[:, -1], "gy", 1)
    return (pressure, vel_x, vel_y, vel_z)


def solution(mesh):
    in_specs = (
        P("gx", "gy", None),
        P("gx", "gy", None),
        P("gx", "gy", None),
        P("gx", "gy", None),
        P("gx", "gy", None),
        P(("gx", "gy"), None, None),
        P(("gx", "gy"), None),
        P(("gx", "gy")),
        P("gx", "gy", None),
        P(),
    )
    out_specs = (P("gx", "gy", None), P("gx", "gy", None), P("gx", "gy", None), P("gx", "gy", None))
    return jax.shard_map(body, mesh=mesh, in_specs=in_specs, out_specs=out_specs, check_vma=False)
```
